512 devices in a mesh: blk: 16 (over x_hi, y, core), wide: 32 (over x_lo, z).
Axes of the slice: x: 4 (x_hi: 2, x_lo: 2; x = x_hi * 2 + x_lo), y: 4, z: 16, core: 2. Of those that a mesh axis runs over, the one named last changes fastest.
Arguments:
- series: bfloat16 [90112, 640], P(('blk', 'wide'))
- scrub_mask: int32 [640], replicated, may hold values from 0 to 1, as said below
- seed_index: int32 [4096], P(('blk', 'wide')), may hold values from 0 to 90111, as said below
Outputs:
- dispersion: bfloat16 [16, 5632, 4096], P(None, 'wide', 'blk')
- statistic: bfloat16 [16, 5632, 4096], P(None, 'wide', 'blk')
The draws below stay inside these ranges and needn't reach their ends.
Inputs may be any that keep to these rules, and one draw needn't show every extreme that they name: Entry i of seed_index lies among the rows (i // 8) * 176 to (i // 8 + 1) * 176 - 1, and the 8 entries of one such block are distinct. `scrub_mask`: every frame of even position is kept.
All inputs are finite; a program needn't handle non-finite values.
Results may differ from the reference program's by a relative error of at most 0.0057.
Values may be sent and summed in bfloat16 or wider, within the bound.
No kernel may reach another device: no remote copies, remote signals or barrier semaphores. Data moves between devices by JAX's collectives and lax.ppermute only.
A program may use at most 128 MiB of HBM per device.

```python
import math
import jax
import jax.numpy as jnp
from jax import lax

SEED_DEV = 8
TGT_DEV = 176
FRAMES = 640
WIN = 60
STRIDE = 30
NWIN = 20
SEEDS = 4096
TARGETS = 90112
N_BLK = 16
N_WIDE = 32


def draw_series(key, part):
    key_scale, key_offset, key_gain, key_noise = jax.random.split(key, 4)
    row_scale = jnp.exp(jax.random.uniform(key_scale, (TARGETS, 1), minval=0.0, maxval=math.log(10.0)))
    offset = jax.random.uniform(key_offset, (TARGETS, 1), minval=-3.0, maxval=3.0)
    frame_gain = jnp.exp(jax.random.uniform(key_gain, (1, FRAMES), minval=-0.7, maxval=0.7))
    fluctuation = jax.random.normal(key_noise, (TARGETS, FRAMES))
    return (offset + row_scale * frame_gain * fluctuation).astype(jnp.bfloat16)


def draw_scrub_mask(key, part):
    coin_flips = jax.random.randint(key, (FRAMES,), 0, 4)
    position = jnp.arange(FRAMES, dtype=jnp.int32)
    return jnp.where((position % 2 == 0) | (coin_flips != 0), 1, 0).astype(jnp.int32)


def pick_block(block_key):
    return jax.random.permutation(block_key, TGT_DEV)[:SEED_DEV]


def draw_seed_index(key, part):
    block_count = SEEDS // SEED_DEV
    block_keys = jax.random.split(key, block_count)
    chosen = jax.vmap(pick_block)(block_keys).astype(jnp.int32)
    offsets = jnp.arange(block_count, dtype=jnp.int32)[:, None] * TGT_DEV
    return (chosen + offsets).reshape(SEEDS).astype(jnp.int32)


def setup_inputs(seed: int = 0) -> dict:
    key_of = jax.random.split(jax.random.key(seed), 4)
    return {
        "series": draw_series(jax.random.fold_in(key_of[3], 71), 0),
        "scrub_mask": draw_scrub_mask(jax.random.fold_in(key_of[3], 71), 0),
        "seed_index": draw_seed_index(jax.random.fold_in(key_of[3], 71), 0),
    }


EPSILON = 1e-05
CLIP_LEVEL = 0.99

def fisher_of(values):
    clipped = jnp.clip(values, -CLIP_LEVEL, CLIP_LEVEL)
    return 0.5 * (jnp.log(1.0 + clipped) - jnp.log(1.0 - clipped))

def prepare(raw_rows, scrub_mask):
    values = raw_rows.astype(jnp.float32)
    row_count = values.shape[0]
    weight = scrub_mask.astype(jnp.float32)
    covered = STRIDE * (NWIN + 1)
    pieces = values[:, :covered].reshape(row_count, NWIN + 1, STRIDE)
    framed = jnp.concatenate([pieces[:, :-1], pieces[:, 1:]], axis=2)
    mask_pieces = weight[:covered].reshape(NWIN + 1, STRIDE)
    mask_framed = jnp.concatenate([mask_pieces[:-1], mask_pieces[1:]], axis=1)
    valid_count = lax.optimization_barrier(jnp.sum(mask_framed, axis=1))
    centre = lax.optimization_barrier(jnp.sum(framed * mask_framed, axis=2)) / valid_count
    centred = (framed - centre[:, :, None]) * mask_framed
    spread = lax.optimization_barrier(jnp.sum(centred * centred, axis=2))
    windows = (centred * lax.rsqrt(spread + EPSILON)[:, :, None]).astype(jnp.bfloat16)
    total_valid = jnp.sum(weight)
    mean_all = lax.optimization_barrier(jnp.sum(values * weight, axis=1)) / total_valid
    centred_all = (values - mean_all[:, None]) * weight
    spread_all = lax.optimization_barrier(jnp.sum(centred_all * centred_all, axis=1))
    whole_std = (centred_all * lax.rsqrt(spread_all + EPSILON)[:, None]).astype(jnp.bfloat16)
    return (windows, whole_std)

def compare_exact(target_windows, target_whole, seed_window, seed_whole, total_valid):
    window_corr = jnp.einsum('tnw,snw->nts', target_windows.astype(jnp.float32), seed_window.astype(jnp.float32), precision=lax.Precision.HIGHEST)
    fisher = fisher_of(window_corr)
    first_moment = lax.optimization_barrier(jnp.mean(fisher, axis=0))
    second = lax.optimization_barrier(jnp.mean(fisher * fisher, axis=0))
    dispersion = ((WIN - 3) * (second - first_moment * first_moment)).astype(jnp.bfloat16)
    static = jnp.einsum('tf,sf->ts', target_whole.astype(jnp.float32), seed_whole.astype(jnp.float32), precision=lax.Precision.HIGHEST)
    statistic = (jnp.sqrt(total_valid - 3.0) * fisher_of(static)).astype(jnp.bfloat16)
    return (dispersion, statistic)

def reference(series, scrub_mask, seed_index):
    target_windows, target_whole = prepare(series, scrub_mask)
    seed_window, seed_whole = prepare(jnp.take(series, seed_index, axis=0), scrub_mask)
    total_valid = jnp.sum(scrub_mask.astype(jnp.float32))
    block_count = TARGETS // TGT_DEV
    grouped_windows = target_windows.reshape(block_count, TGT_DEV, NWIN, WIN)
    grouped_whole = target_whole.reshape(block_count, TGT_DEV, FRAMES)

    def compare_block(block_pair):
        return compare_exact(block_pair[0], block_pair[1], seed_window, seed_whole, total_valid)
    dispersion, statistic = lax.map(compare_block, (grouped_windows, grouped_whole))
    out_shape = (N_BLK, N_WIDE * TGT_DEV, SEEDS)
    return (dispersion.reshape(out_shape), statistic.reshape(out_shape))
```

```python
import jax
import jax.numpy as jnp
from jax import lax
from jax.sharding import PartitionSpec as P

WIN = 60
STRIDE = 30
NWIN = 20


EPSILON = 1e-05
CLIP_LEVEL = 0.99


def fisher_of(values):
    clipped = jnp.clip(values, -CLIP_LEVEL, CLIP_LEVEL)
    return 0.5 * (jnp.log(1.0 + clipped) - jnp.log(1.0 - clipped))


def prepare(raw_rows, scrub_mask):
    values = raw_rows.astype(jnp.float32)
    row_count = values.shape[0]
    weight = scrub_mask.astype(jnp.float32)
    covered = STRIDE * (NWIN + 1)
    pieces = values[:, :covered].reshape(row_count, NWIN + 1, STRIDE)
    framed = jnp.concatenate([pieces[:, :-1], pieces[:, 1:]], axis=2)
    mask_pieces = weight[:covered].reshape(NWIN + 1, STRIDE)
    mask_framed = jnp.concatenate([mask_pieces[:-1], mask_pieces[1:]], axis=1)
    valid_count = jnp.sum(mask_framed, axis=1)
    centre = jnp.sum(framed * mask_framed, axis=2) / valid_count
    centred = (framed - centre[:, :, None]) * mask_framed
    spread = jnp.sum(centred * centred, axis=2)
    windows = (centred * lax.rsqrt(spread + EPSILON)[:, :, None]).astype(jnp.bfloat16)
    total_valid = jnp.sum(weight)
    mean_all = jnp.sum(values * weight, axis=1) / total_valid
    centred_all = (values - mean_all[:, None]) * weight
    spread_all = jnp.sum(centred_all * centred_all, axis=1)
    whole_std = (centred_all * lax.rsqrt(spread_all + EPSILON)[:, None]).astype(jnp.bfloat16)
    return (windows, whole_std)


def compare(target_windows, target_whole, seed_window, seed_whole, total_valid):
    window_corr = jnp.einsum(
        "tnw,snw->nts", target_windows, seed_window, preferred_element_type=jnp.float32
    )
    fisher = fisher_of(window_corr)
    first_moment = jnp.mean(fisher, axis=0)
    second = jnp.mean(fisher * fisher, axis=0)
    dispersion = ((WIN - 3) * (second - first_moment * first_moment)).astype(jnp.bfloat16)
    static = jnp.einsum("tf,sf->ts", target_whole, seed_whole, preferred_element_type=jnp.float32)
    statistic = (jnp.sqrt(total_valid - 3.0) * fisher_of(static)).astype(jnp.bfloat16)
    return (dispersion, statistic)


def body(series, scrub_mask, seed_index):
    row_count, frames = series.shape
    local_rows = seed_index % row_count
    own_seeds = jnp.take(series, local_rows, axis=0)
    total_valid = jnp.sum(scrub_mask.astype(jnp.float32))
    panel_rows = lax.all_gather(own_seeds, "wide", axis=0, tiled=True)
    seed_window, seed_whole = prepare(panel_rows, scrub_mask)
    blocks = lax.axis_size("blk")
    gathered = lax.all_gather(series, "blk", axis=0, tiled=True)
    target_windows, target_whole = prepare(gathered, scrub_mask)
    dispersion, statistic = compare(
        target_windows, target_whole, seed_window, seed_whole, total_valid
    )
    shape = (blocks, row_count, panel_rows.shape[0])
    return (dispersion.reshape(shape), statistic.reshape(shape))


def solution(mesh):
    in_specs = (P(("blk", "wide"), None), P(), P(("blk", "wide")))
    out_specs = (P(None, "wide", "blk"), P(None, "wide", "blk"))
    return jax.shard_map(body, mesh=mesh, in_specs=in_specs, out_specs=out_specs, check_vma=False)
```

```python
import functools

import numpy as np
import jax
import jax.numpy as jnp
from jax import lax
from jax.experimental import pallas as pl
from jax.experimental.pallas import tpu as pltpu
from jax.sharding import PartitionSpec as P

WIN = 60
STRIDE = 30
NWIN = 20
LANES = 128
SPAN = 256


EPSILON = 1e-05
CLIP_LEVEL = 0.99


def fisher_of(values):
    clipped = jnp.clip(values, -CLIP_LEVEL, CLIP_LEVEL)
    return 0.5 * (jnp.log(1.0 + clipped) - jnp.log(1.0 - clipped))


def window_frames(frames):
    out = []
    for n in range(NWIN):
        start = LANES * ((STRIDE * n) // LANES)
        out.append((start, min(SPAN, frames - start)))
    return out


def prepare(raw_rows, scrub_mask):
    values = raw_rows.astype(jnp.float32)
    row_count = values.shape[0]
    weight = scrub_mask.astype(jnp.float32)
    covered = STRIDE * (NWIN + 1)
    pieces = values[:, :covered].reshape(row_count, NWIN + 1, STRIDE)
    framed = jnp.concatenate([pieces[:, :-1], pieces[:, 1:]], axis=2)
    mask_pieces = weight[:covered].reshape(NWIN + 1, STRIDE)
    mask_framed = jnp.concatenate([mask_pieces[:-1], mask_pieces[1:]], axis=1)
    valid_count = jnp.sum(mask_framed, axis=1)
    centre = jnp.sum(framed * mask_framed, axis=2) / valid_count
    centred = (framed - centre[:, :, None]) * mask_framed
    spread = jnp.sum(centred * centred, axis=2)
    windows = (centred * lax.rsqrt(spread + EPSILON)[:, :, None]).astype(jnp.bfloat16)
    total_valid = jnp.sum(weight)
    mean_all = jnp.sum(values * weight, axis=1) / total_valid
    centred_all = (values - mean_all[:, None]) * weight
    spread_all = jnp.sum(centred_all * centred_all, axis=1)
    whole_std = (centred_all * lax.rsqrt(spread_all + EPSILON)[:, None]).astype(jnp.bfloat16)
    return (windows, whole_std)


def seed_operands(seed_window, seed_whole, frames):
    blocks = []
    for n, (start, width) in enumerate(window_frames(frames)):
        left = STRIDE * n - start
        part = seed_window[:, n, :]
        part = jnp.pad(part, ((0, 0), (left, SPAN - WIN - left)))
        blocks.append(part.T)
    return jnp.stack(blocks), seed_whole.T


def window_masks(weight, frames):
    rows = []
    for n, (start, width) in enumerate(window_frames(frames)):
        local = np.arange(SPAN) + start
        inside = (local >= STRIDE * n) & (local < STRIDE * n + WIN) & (local < frames)
        idx = np.minimum(local, frames - 1)
        rows.append(jnp.where(jnp.asarray(inside), weight[idx], 0.0))
    return jnp.stack(rows)


def compare_kernel(x_ref, m_ref, mw_ref, sw_ref, sh_ref, disp_ref, stat_ref):
    frames = x_ref.shape[1]
    x = x_ref[...].astype(jnp.float32)
    m = m_ref[...]
    total_valid = jnp.sum(m)
    mean_all = jnp.sum(x * m, axis=1, keepdims=True) / total_valid
    centred = (x - mean_all) * m
    spread = jnp.sum(centred * centred, axis=1, keepdims=True)
    whole = (centred * lax.rsqrt(spread + EPSILON)).astype(jnp.bfloat16)
    q = jnp.dot(whole, sh_ref[...], preferred_element_type=jnp.float32)
    stat_ref[...] = (jnp.sqrt(total_valid - 3.0) * fisher_of(q)).astype(stat_ref.dtype)
    first = None
    second = None
    for n, (start, width) in enumerate(window_frames(frames)):
        xw = x[:, start:start + width]
        mw = mw_ref[n:n + 1, :width]
        count = jnp.sum(mw)
        centre = jnp.sum(xw * mw, axis=1, keepdims=True) / count
        cw = (xw - centre) * mw
        sp = jnp.sum(cw * cw, axis=1, keepdims=True)
        w = (cw * lax.rsqrt(sp + EPSILON)).astype(jnp.bfloat16)
        r = jnp.dot(w, sw_ref[n, :width, :], preferred_element_type=jnp.float32)
        z = fisher_of(r)
        if first is None:
            first, second = z, z * z
        else:
            first, second = first + z, second + z * z
    first = first / NWIN
    second = second / NWIN
    disp_ref[...] = ((WIN - 3) * (second - first * first)).astype(disp_ref.dtype)


def compare_rows(rows, weight, seed_window, seed_whole, block):
    count, frames = rows.shape
    seeds = seed_whole.shape[0]
    sw, sh = seed_operands(seed_window, seed_whole, frames)
    mw = window_masks(weight, frames)
    steps = count // block
    flops = 2 * count * seeds * (frames + NWIN * SPAN)
    cost = pl.CostEstimate(
        flops=flops,
        transcendentals=2 * count * seeds * (NWIN + 1),
        bytes_accessed=count * frames * 2 + sw.size * 2 + 2 * count * seeds * 2,
    )
    out = jax.ShapeDtypeStruct((count, seeds), jnp.bfloat16)
    return pl.pallas_call(
        compare_kernel,
        grid=(steps,),
        in_specs=[
            pl.BlockSpec((block, frames), lambda i: (i, 0)),
            pl.BlockSpec((1, frames), lambda i: (0, 0)),
            pl.BlockSpec((NWIN, SPAN), lambda i: (0, 0)),
            pl.BlockSpec((NWIN, SPAN, seeds), lambda i: (0, 0, 0)),
            pl.BlockSpec((frames, seeds), lambda i: (0, 0)),
        ],
        out_specs=[
            pl.BlockSpec((block, seeds), lambda i: (i, 0)),
            pl.BlockSpec((block, seeds), lambda i: (i, 0)),
        ],
        out_shape=[out, out],
        cost_estimate=cost,
        compiler_params=pltpu.CompilerParams(vmem_limit_bytes=48 * 1024 * 1024),
    )(rows, weight[None, :], mw, sw, sh)


def body(series, scrub_mask, seed_index):
    row_count, frames = series.shape
    local_rows = seed_index % row_count
    own_seeds = jnp.take(series, local_rows, axis=0)
    weight = scrub_mask.astype(jnp.float32)
    panel_rows = lax.all_gather(own_seeds, "wide", axis=0, tiled=True)
    seed_window, seed_whole = prepare(panel_rows, scrub_mask)
    blocks = lax.axis_size("blk")
    gathered = lax.all_gather(series, "blk", axis=0, tiled=True)
    dispersion, statistic = compare_rows(gathered, weight, seed_window, seed_whole, row_count)
    shape = (blocks, row_count, panel_rows.shape[0])
    return (dispersion.reshape(shape), statistic.reshape(shape))


def solution(mesh):
    in_specs = (P(("blk", "wide"), None), P(), P(("blk", "wide")))
    out_specs = (P(None, "wide", "blk"), P(None, "wide", "blk"))
    return jax.shard_map(body, mesh=mesh, in_specs=in_specs, out_specs=out_specs, check_vma=False)
```

```python
import numpy as np
import jax
import jax.numpy as jnp
from jax import lax
from jax.experimental import pallas as pl
from jax.experimental.pallas import tpu as pltpu
from jax.sharding import PartitionSpec as P

WIN = 60
STRIDE = 30
NWIN = 20
LANES = 128
SPAN = 256
ROW_TILE = 16


EPSILON = 1e-05
CLIP_LEVEL = 0.99


def fisher_of(values):
    clipped = jnp.clip(values, -CLIP_LEVEL, CLIP_LEVEL)
    return 0.5 * (jnp.log(1.0 + clipped) - jnp.log(1.0 - clipped))


def window_frames(frames):
    out = []
    for n in range(NWIN):
        start = LANES * ((STRIDE * n) // LANES)
        out.append((start, min(SPAN, frames - start)))
    return out


def prepare(raw_rows, scrub_mask):
    values = raw_rows.astype(jnp.float32)
    row_count = values.shape[0]
    weight = scrub_mask.astype(jnp.float32)
    covered = STRIDE * (NWIN + 1)
    pieces = values[:, :covered].reshape(row_count, NWIN + 1, STRIDE)
    framed = jnp.concatenate([pieces[:, :-1], pieces[:, 1:]], axis=2)
    mask_pieces = weight[:covered].reshape(NWIN + 1, STRIDE)
    mask_framed = jnp.concatenate([mask_pieces[:-1], mask_pieces[1:]], axis=1)
    valid_count = jnp.sum(mask_framed, axis=1)
    centre = jnp.sum(framed * mask_framed, axis=2) / valid_count
    centred = (framed - centre[:, :, None]) * mask_framed
    spread = jnp.sum(centred * centred, axis=2)
    windows = (centred * lax.rsqrt(spread + EPSILON)[:, :, None]).astype(jnp.bfloat16)
    total_valid = jnp.sum(weight)
    mean_all = jnp.sum(values * weight, axis=1) / total_valid
    centred_all = (values - mean_all[:, None]) * weight
    spread_all = jnp.sum(centred_all * centred_all, axis=1)
    whole_std = (centred_all * lax.rsqrt(spread_all + EPSILON)[:, None]).astype(jnp.bfloat16)
    return (windows, whole_std)


def seed_operands(seed_window, seed_whole, frames):
    blocks = []
    for n, (start, width) in enumerate(window_frames(frames)):
        left = STRIDE * n - start
        part = seed_window[:, n, :]
        part = jnp.pad(part, ((0, 0), (left, SPAN - WIN - left)))
        blocks.append(part.T)
    return jnp.stack(blocks), seed_whole.T


def window_masks(weight, frames):
    padded = jnp.pad(weight, (0, SPAN))
    rows = []
    for n, (start, width) in enumerate(window_frames(frames)):
        local = np.arange(SPAN) + start
        inside = (local >= STRIDE * n) & (local < STRIDE * n + WIN)
        rows.append(padded[start:start + SPAN] * inside.astype(np.float32))
    return jnp.stack(rows)


def compare_kernel(x_ref, m_ref, mw_ref, sw_ref, sh_ref, disp_ref, stat_ref):
    frames = x_ref.shape[1]
    x = x_ref[...].astype(jnp.float32)
    m = m_ref[...]
    total_valid = jnp.sum(m)
    mean_all = jnp.sum(x * m, axis=1, keepdims=True) / total_valid
    centred = (x - mean_all) * m
    spread = jnp.sum(centred * centred, axis=1, keepdims=True)
    whole = (centred * lax.rsqrt(spread + EPSILON)).astype(jnp.bfloat16)
    q = jnp.dot(whole, sh_ref[...], preferred_element_type=jnp.float32)
    stat_ref[...] = (jnp.sqrt(total_valid - 3.0) * fisher_of(q)).astype(stat_ref.dtype)
    first = None
    second = None
    for n, (start, width) in enumerate(window_frames(frames)):
        xw = x[:, start:start + width]
        mw = mw_ref[n:n + 1, :width]
        count = jnp.sum(mw)
        centre = jnp.sum(xw * mw, axis=1, keepdims=True) / count
        cw = (xw - centre) * mw
        sp = jnp.sum(cw * cw, axis=1, keepdims=True)
        w = (cw * lax.rsqrt(sp + EPSILON)).astype(jnp.bfloat16)
        r = jnp.dot(w, sw_ref[n, :width, :], preferred_element_type=jnp.float32)
        z = fisher_of(r)
        if first is None:
            first, second = z, z * z
        else:
            first, second = first + z, second + z * z
    first = first / NWIN
    second = second / NWIN
    disp_ref[...] = ((WIN - 3) * (second - first * first)).astype(disp_ref.dtype)


def compare_rows(rows, m, mw, sw, sh, block):
    count, frames = rows.shape
    seeds = sh.shape[1]
    steps = count // block
    cost = pl.CostEstimate(
        flops=2 * count * seeds * (frames + NWIN * SPAN),
        transcendentals=2 * count * seeds * (NWIN + 1),
        bytes_accessed=count * frames * 2 + sw.size * 2 + 2 * count * seeds * 2,
    )
    out = jax.ShapeDtypeStruct((count, seeds), jnp.bfloat16)
    return pl.pallas_call(
        compare_kernel,
        grid=(steps,),
        in_specs=[
            pl.BlockSpec((block, frames), lambda i: (i, 0)),
            pl.BlockSpec((1, frames), lambda i: (0, 0)),
            pl.BlockSpec((NWIN, SPAN), lambda i: (0, 0)),
            pl.BlockSpec((NWIN, SPAN, seeds), lambda i: (0, 0, 0)),
            pl.BlockSpec((frames, seeds), lambda i: (0, 0)),
        ],
        out_specs=[
            pl.BlockSpec((block, seeds), lambda i: (i, 0)),
            pl.BlockSpec((block, seeds), lambda i: (i, 0)),
        ],
        out_shape=[out, out],
        cost_estimate=cost,
        compiler_params=pltpu.CompilerParams(vmem_limit_bytes=48 * 1024 * 1024),
    )(rows, m, mw, sw, sh)


def doubling_gather(block, axis):
    size = lax.axis_size(axis)
    me = lax.axis_index(axis)
    bits = size.bit_length() - 1
    low = list(range(bits - 1))[::-1]
    order = low + [bits - 1] if bits > 1 else [0]
    held = block[None]
    for bit in order:
        stride = 1 << bit
        route = [(i, i ^ stride) for i in range(size)]
        other = lax.ppermute(held, axis, route)
        mine_low = ((me >> bit) & 1) == 0
        held = jnp.where(mine_low, jnp.stack([held, other]), jnp.stack([other, held]))
    placed = order[::-1]
    perm = [placed.index(bits - 1 - j) for j in range(bits)]
    held = held.reshape((2,) * bits + block.shape)
    held = jnp.transpose(held, perm + [bits + k for k in range(block.ndim)])
    return held.reshape((size * block.shape[0],) + block.shape[1:])


def row_chunks(row_count):
    tiles = row_count // ROW_TILE
    counts = [tiles // 2 + (1 if k < tiles % 2 else 0) for k in range(2)]
    out, start = [], 0
    for c in counts:
        out.append((start * ROW_TILE, c * ROW_TILE))
        start += c
    return out


def body(series, scrub_mask, seed_index):
    row_count, frames = series.shape
    local_rows = seed_index % row_count
    own_seeds = jnp.take(series, local_rows, axis=0)
    weight = scrub_mask.astype(jnp.float32)
    blocks = lax.axis_size("blk")
    gathered = [
        lax.all_gather(series[start:start + n], "blk", axis=0, tiled=True)
        for start, n in row_chunks(row_count)
    ]
    panel_rows = doubling_gather(own_seeds, "wide")
    seed_window, seed_whole = prepare(panel_rows, scrub_mask)
    sw, sh = seed_operands(seed_window, seed_whole, frames)
    mw = window_masks(weight, frames)
    seeds = panel_rows.shape[0]
    parts_d, parts_s = [], []
    for (start, n), rows in zip(row_chunks(row_count), gathered):
        d, s = compare_rows(rows, weight[None, :], mw, sw, sh, n)
        parts_d.append(d.reshape(blocks, n, seeds))
        parts_s.append(s.reshape(blocks, n, seeds))
    return (jnp.concatenate(parts_d, axis=1), jnp.concatenate(parts_s, axis=1))


def solution(mesh):
    in_specs = (P(("blk", "wide"), None), P(), P(("blk", "wide")))
    out_specs = (P(None, "wide", "blk"), P(None, "wide", "blk"))
    return jax.shard_map(body, mesh=mesh, in_specs=in_specs, out_specs=out_specs, check_vma=False)
```

```python
import numpy as np
import jax
import jax.numpy as jnp
from jax import lax
from jax.experimental import pallas as pl
from jax.experimental.pallas import tpu as pltpu
from jax.sharding import PartitionSpec as P

WIN = 60
STRIDE = 30
NWIN = 20
LANES = 128
SPAN = 256
ROW_TILE = 16


EPSILON = 1e-05
CLIP_LEVEL = 0.99


def fisher_of(values):
    clipped = jnp.clip(values, -CLIP_LEVEL, CLIP_LEVEL)
    return 0.5 * (jnp.log(1.0 + clipped) - jnp.log(1.0 - clipped))


def window_frames(frames):
    out = []
    for n in range(NWIN):
        start = LANES * ((STRIDE * n) // LANES)
        out.append((start, min(SPAN, frames - start)))
    return out


def prepare(raw_rows, scrub_mask):
    values = raw_rows.astype(jnp.float32)
    row_count = values.shape[0]
    weight = scrub_mask.astype(jnp.float32)
    covered = STRIDE * (NWIN + 1)
    pieces = values[:, :covered].reshape(row_count, NWIN + 1, STRIDE)
    framed = jnp.concatenate([pieces[:, :-1], pieces[:, 1:]], axis=2)
    mask_pieces = weight[:covered].reshape(NWIN + 1, STRIDE)
    mask_framed = jnp.concatenate([mask_pieces[:-1], mask_pieces[1:]], axis=1)
    valid_count = jnp.sum(mask_framed, axis=1)
    centre = jnp.sum(framed * mask_framed, axis=2) / valid_count
    centred = (framed - centre[:, :, None]) * mask_framed
    spread = jnp.sum(centred * centred, axis=2)
    windows = (centred * lax.rsqrt(spread + EPSILON)[:, :, None]).astype(jnp.bfloat16)
    total_valid = jnp.sum(weight)
    mean_all = jnp.sum(values * weight, axis=1) / total_valid
    centred_all = (values - mean_all[:, None]) * weight
    spread_all = jnp.sum(centred_all * centred_all, axis=1)
    whole_std = (centred_all * lax.rsqrt(spread_all + EPSILON)[:, None]).astype(jnp.bfloat16)
    return (windows, whole_std)


def seed_operands(seed_window, seed_whole, frames):
    blocks = []
    for n, (start, width) in enumerate(window_frames(frames)):
        left = STRIDE * n - start
        part = seed_window[:, n, :]
        part = jnp.pad(part, ((0, 0), (left, SPAN - WIN - left)))
        blocks.append(part.T)
    return jnp.stack(blocks), seed_whole.T


def window_masks(weight, frames):
    padded = jnp.pad(weight, (0, SPAN))
    rows = []
    for n, (start, width) in enumerate(window_frames(frames)):
        local = np.arange(SPAN) + start
        inside = (local >= STRIDE * n) & (local < STRIDE * n + WIN)
        rows.append(padded[start:start + SPAN] * inside.astype(np.float32))
    return jnp.stack(rows)


def compare_kernel(x_ref, m_ref, mw_ref, sw_ref, sh_ref, disp_ref, stat_ref):
    frames = x_ref.shape[1]
    x = x_ref[...].astype(jnp.float32)
    m = m_ref[...]
    total_valid = jnp.sum(m)
    mean_all = jnp.sum(x * m, axis=1, keepdims=True) / total_valid
    centred = (x - mean_all) * m
    spread = jnp.sum(centred * centred, axis=1, keepdims=True)
    whole = (centred * lax.rsqrt(spread + EPSILON)).astype(jnp.bfloat16)
    q = jnp.dot(whole, sh_ref[...], preferred_element_type=jnp.float32)
    stat_ref[...] = (jnp.sqrt(total_valid - 3.0) * fisher_of(q)).astype(stat_ref.dtype)
    first = None
    second = None
    for n, (start, width) in enumerate(window_frames(frames)):
        xw = x[:, start:start + width]
        mw = mw_ref[n:n + 1, :width]
        count = jnp.sum(mw)
        centre = jnp.sum(xw * mw, axis=1, keepdims=True) / count
        cw = (xw - centre) * mw
        sp = jnp.sum(cw * cw, axis=1, keepdims=True)
        w = (cw * lax.rsqrt(sp + EPSILON)).astype(jnp.bfloat16)
        r = jnp.dot(w, sw_ref[n, :width, :], preferred_element_type=jnp.float32)
        z = fisher_of(r)
        if first is None:
            first, second = z, z * z
        else:
            first, second = first + z, second + z * z
    first = first / NWIN
    second = second / NWIN
    disp_ref[...] = ((WIN - 3) * (second - first * first)).astype(disp_ref.dtype)


def compare_rows(rows, m, mw, sw, sh, block):
    count, frames = rows.shape
    seeds = sh.shape[1]
    steps = count // block
    cost = pl.CostEstimate(
        flops=2 * count * seeds * (frames + NWIN * SPAN),
        transcendentals=2 * count * seeds * (NWIN + 1),
        bytes_accessed=count * frames * 2 + sw.size * 2 + 2 * count * seeds * 2,
    )
    out = jax.ShapeDtypeStruct((count, seeds), jnp.bfloat16)
    return pl.pallas_call(
        compare_kernel,
        grid=(steps,),
        in_specs=[
            pl.BlockSpec((block, frames), lambda i: (i, 0)),
            pl.BlockSpec((1, frames), lambda i: (0, 0)),
            pl.BlockSpec((NWIN, SPAN), lambda i: (0, 0)),
            pl.BlockSpec((NWIN, SPAN, seeds), lambda i: (0, 0, 0)),
            pl.BlockSpec((frames, seeds), lambda i: (0, 0)),
        ],
        out_specs=[
            pl.BlockSpec((block, seeds), lambda i: (i, 0)),
            pl.BlockSpec((block, seeds), lambda i: (i, 0)),
        ],
        out_shape=[out, out],
        cost_estimate=cost,
        compiler_params=pltpu.CompilerParams(vmem_limit_bytes=48 * 1024 * 1024),
    )(rows, m, mw, sw, sh)


def doubling_gather(block, axis):
    size = lax.axis_size(axis)
    me = lax.axis_index(axis)
    bits = size.bit_length() - 1
    low = list(range(bits - 1))[::-1]
    order = low + [bits - 1] if bits > 1 else [0]
    held = block[None]
    for bit in order:
        stride = 1 << bit
        route = [(i, i ^ stride) for i in range(size)]
        other = lax.ppermute(held, axis, route)
        held = place_pair(held, other, me, bit)
    return unpermute(held, order, size, block)


def place_pair(held, other, me, bit):
    mine_low = ((me >> bit) & 1) == 0
    return jnp.where(mine_low, jnp.stack([held, other]), jnp.stack([other, held]))


def unpermute(held, order, size, block):
    bits = len(order)
    placed = order[::-1]
    perm = [placed.index(bits - 1 - j) for j in range(bits)]
    held = held.reshape((2,) * bits + block.shape)
    held = jnp.transpose(held, perm + [bits + k for k in range(block.ndim)])
    return held.reshape((size * block.shape[0],) + block.shape[1:])


BLK_AXES = ("x_hi", "y", "core")
WIDE_AXES = ("x_lo", "z")


def body(series, scrub_mask, seed_index):
    row_count, frames = series.shape
    local_rows = seed_index % row_count
    own_seeds = jnp.take(series, local_rows, axis=0)
    weight = scrub_mask.astype(jnp.float32)
    panel_rows = lax.all_gather(own_seeds, "z", axis=0, tiled=True)
    panel_rows = lax.all_gather(panel_rows, "x_lo", axis=0, tiled=True)
    seed_window, seed_whole = prepare(panel_rows, scrub_mask)
    sw, sh = seed_operands(seed_window, seed_whole, frames)
    mw = window_masks(weight, frames)
    m = weight[None, :]
    seeds = panel_rows.shape[0]
    size = 1
    for a in BLK_AXES:
        size *= lax.axis_size(a)
    me = lax.axis_index(BLK_AXES)
    bits = size.bit_length() - 1
    order = list(range(bits))[::-1]

    def run(rows):
        count = rows.shape[0] * rows.shape[1]
        d, s = compare_rows(rows.reshape(count, frames), m, mw, sw, sh, row_count)
        return d.reshape(rows.shape[0], row_count, seeds), s.reshape(rows.shape[0], row_count, seeds)

    held = series[None]
    held_d, held_s = run(held)
    for bit in order:
        stride = 1 << bit
        route = [(i, i ^ stride) for i in range(size)]
        other = lax.ppermute(held, BLK_AXES, route)
        other_d, other_s = run(other)
        held = place_pair(held, other, me, bit)
        held_d = place_pair(held_d, other_d, me, bit)
        held_s = place_pair(held_s, other_s, me, bit)
        shape = (-1,) + series.shape
        held = held.reshape(shape)
        held_d = held_d.reshape((-1, row_count, seeds))
        held_s = held_s.reshape((-1, row_count, seeds))
    out_block = jnp.zeros((row_count, seeds), jnp.bfloat16)
    dispersion = unpermute(held_d.reshape((2,) * bits + (row_count, seeds)), order, size, out_block)
    statistic = unpermute(held_s.reshape((2,) * bits + (row_count, seeds)), order, size, out_block)
    return (dispersion.reshape(size, row_count, seeds), statistic.reshape(size, row_count, seeds))


def solution(mesh):
    from jax.sharding import Mesh
    split = Mesh(mesh.devices.reshape(2, 4, 2, 2, 16), BLK_AXES + WIDE_AXES)
    every = BLK_AXES + WIDE_AXES
    in_specs = (P(every, None), P(), P(every))
    out_specs = (P(None, WIDE_AXES, BLK_AXES), P(None, WIDE_AXES, BLK_AXES))
    return jax.shard_map(body, mesh=split, in_specs=in_specs, out_specs=out_specs, check_vma=False)
```

```python
import numpy as np
import jax
import jax.numpy as jnp
from jax import lax
from jax.experimental import pallas as pl
from jax.experimental.pallas import tpu as pltpu
from jax.sharding import PartitionSpec as P

WIN = 60
STRIDE = 30
NWIN = 20
LANES = 128
SPAN = 256
ROW_TILE = 16


EPSILON = 1e-05
CLIP_LEVEL = 0.99


def fisher_of(values):
    clipped = jnp.clip(values, -CLIP_LEVEL, CLIP_LEVEL)
    return 0.5 * (jnp.log(1.0 + clipped) - jnp.log(1.0 - clipped))


def window_frames(frames):
    out = []
    for n in range(NWIN):
        start = LANES * ((STRIDE * n) // LANES)
        width = LANES if STRIDE * n - start + WIN <= LANES else SPAN
        out.append((start, min(width, frames - start)))
    return out


def prepare(raw_rows, scrub_mask):
    values = raw_rows.astype(jnp.float32)
    row_count = values.shape[0]
    weight = scrub_mask.astype(jnp.float32)
    covered = STRIDE * (NWIN + 1)
    pieces = values[:, :covered].reshape(row_count, NWIN + 1, STRIDE)
    framed = jnp.concatenate([pieces[:, :-1], pieces[:, 1:]], axis=2)
    mask_pieces = weight[:covered].reshape(NWIN + 1, STRIDE)
    mask_framed = jnp.concatenate([mask_pieces[:-1], mask_pieces[1:]], axis=1)
    valid_count = jnp.sum(mask_framed, axis=1)
    centre = jnp.sum(framed * mask_framed, axis=2) / valid_count
    centred = (framed - centre[:, :, None]) * mask_framed
    spread = jnp.sum(centred * centred, axis=2)
    windows = (centred * lax.rsqrt(spread + EPSILON)[:, :, None]).astype(jnp.bfloat16)
    total_valid = jnp.sum(weight)
    mean_all = jnp.sum(values * weight, axis=1) / total_valid
    centred_all = (values - mean_all[:, None]) * weight
    spread_all = jnp.sum(centred_all * centred_all, axis=1)
    whole_std = (centred_all * lax.rsqrt(spread_all + EPSILON)[:, None]).astype(jnp.bfloat16)
    return (windows, whole_std)


def seed_operands(seed_window, seed_whole, frames):
    blocks = []
    for n, (start, width) in enumerate(window_frames(frames)):
        left = STRIDE * n - start
        part = seed_window[:, n, :]
        part = jnp.pad(part, ((0, 0), (left, SPAN - WIN - left)))
        blocks.append(part.T)
    return jnp.stack(blocks), seed_whole.T


def window_masks(weight, frames):
    padded = jnp.pad(weight, (0, SPAN))
    rows = []
    for n, (start, width) in enumerate(window_frames(frames)):
        local = np.arange(SPAN) + start
        inside = (local >= STRIDE * n) & (local < STRIDE * n + WIN)
        rows.append(padded[start:start + SPAN] * inside.astype(np.float32))
    return jnp.stack(rows)


def fisher_ratio(values):
    clipped = jnp.clip(values, -CLIP_LEVEL, CLIP_LEVEL)
    return 0.5 * jnp.log((1.0 + clipped) / (1.0 - clipped))


def compare_kernel(x_ref, m_ref, mw_ref, sw_ref, sh_ref, disp_ref, stat_ref):
    frames = x_ref.shape[1]
    x = x_ref[...].astype(jnp.float32)
    m = m_ref[...]
    total_valid = jnp.sum(m)
    mean_all = jnp.sum(x * m, axis=1, keepdims=True) / total_valid
    centred = (x - mean_all) * m
    spread = jnp.sum(centred * centred, axis=1, keepdims=True)
    whole = (centred * lax.rsqrt(spread + EPSILON)).astype(jnp.bfloat16)
    q = jnp.dot(whole, sh_ref[...], preferred_element_type=jnp.float32)
    stat_ref[...] = (jnp.sqrt(total_valid - 3.0) * fisher_of(q)).astype(stat_ref.dtype)
    first = None
    second = None
    for n, (start, width) in enumerate(window_frames(frames)):
        xw = x[:, start:start + width]
        mw = mw_ref[n:n + 1, :width]
        count = jnp.sum(mw)
        centre = jnp.sum(xw * mw, axis=1, keepdims=True) / count
        cw = (xw - centre) * mw
        sp = jnp.sum(cw * cw, axis=1, keepdims=True)
        w = (cw * lax.rsqrt(sp + EPSILON)).astype(jnp.bfloat16)
        r = jnp.dot(w, sw_ref[n, :width, :], preferred_element_type=jnp.float32)
        z = fisher_ratio(r)
        if first is None:
            first, second = z, z * z
        else:
            first, second = first + z, second + z * z
    first = first / NWIN
    second = second / NWIN
    disp_ref[...] = ((WIN - 3) * (second - first * first)).astype(disp_ref.dtype)


def compare_rows(rows, m, mw, sw, sh, block):
    count, frames = rows.shape
    seeds = sh.shape[1]
    steps = count // block
    cost = pl.CostEstimate(
        flops=2 * count * seeds * (frames + NWIN * SPAN),
        transcendentals=2 * count * seeds * (NWIN + 1),
        bytes_accessed=count * frames * 2 + sw.size * 2 + 2 * count * seeds * 2,
    )
    out = jax.ShapeDtypeStruct((count, seeds), jnp.bfloat16)
    return pl.pallas_call(
        compare_kernel,
        grid=(steps,),
        in_specs=[
            pl.BlockSpec((block, frames), lambda i: (i, 0)),
            pl.BlockSpec((1, frames), lambda i: (0, 0)),
            pl.BlockSpec((NWIN, SPAN), lambda i: (0, 0)),
            pl.BlockSpec((NWIN, SPAN, seeds), lambda i: (0, 0, 0)),
            pl.BlockSpec((frames, seeds), lambda i: (0, 0)),
        ],
        out_specs=[
            pl.BlockSpec((block, seeds), lambda i: (i, 0)),
            pl.BlockSpec((block, seeds), lambda i: (i, 0)),
        ],
        out_shape=[out, out],
        cost_estimate=cost,
        compiler_params=pltpu.CompilerParams(vmem_limit_bytes=48 * 1024 * 1024),
    )(rows, m, mw, sw, sh)


def doubling_gather(block, axis):
    size = lax.axis_size(axis)
    me = lax.axis_index(axis)
    bits = size.bit_length() - 1
    low = list(range(bits - 1))[::-1]
    order = low + [bits - 1] if bits > 1 else [0]
    held = block[None]
    for bit in order:
        stride = 1 << bit
        route = [(i, i ^ stride) for i in range(size)]
        other = lax.ppermute(held, axis, route)
        held = place_pair(held, other, me, bit)
    return unpermute(held, order, size, block)


def place_pair(held, other, me, bit):
    mine_low = ((me >> bit) & 1) == 0
    return jnp.where(mine_low, jnp.stack([held, other]), jnp.stack([other, held]))


def unpermute(held, order, size, block):
    bits = len(order)
    placed = order[::-1]
    perm = [placed.index(bits - 1 - j) for j in range(bits)]
    held = held.reshape((2,) * bits + block.shape)
    held = jnp.transpose(held, perm + [bits + k for k in range(block.ndim)])
    return held.reshape((size * block.shape[0],) + block.shape[1:])


BLK_AXES = ("x_hi", "y", "core")
WIDE_AXES = ("x_lo", "z")


def body(series, scrub_mask, seed_index):
    row_count, frames = series.shape
    local_rows = seed_index % row_count
    own_seeds = jnp.take(series, local_rows, axis=0)
    weight = scrub_mask.astype(jnp.float32)
    panel_rows = lax.all_gather(own_seeds, "z", axis=0, tiled=True)
    panel_rows = lax.all_gather(panel_rows, "x_lo", axis=0, tiled=True)
    seed_window, seed_whole = prepare(panel_rows, scrub_mask)
    sw, sh = seed_operands(seed_window, seed_whole, frames)
    mw = window_masks(weight, frames)
    m = weight[None, :]
    seeds = panel_rows.shape[0]
    size = 1
    for a in BLK_AXES:
        size *= lax.axis_size(a)
    me = lax.axis_index(BLK_AXES)
    bits = size.bit_length() - 1
    order = list(range(bits))[::-1]

    def run(rows):
        count = rows.shape[0] * rows.shape[1]
        d, s = compare_rows(rows.reshape(count, frames), m, mw, sw, sh, row_count)
        return d.reshape(rows.shape[0], row_count, seeds), s.reshape(rows.shape[0], row_count, seeds)

    held = series[None]
    outs = [run(held)]
    for idx, bit in enumerate(order):
        stride = 1 << bit
        route = [(i, i ^ stride) for i in range(size)]
        if idx > 0:
            held, prev_d, prev_s = lax.optimization_barrier((held,) + outs[idx - 1])
            outs[idx - 1] = (prev_d, prev_s)
        other = lax.ppermute(held, BLK_AXES, route)
        outs.append(run(other))
        held = place_pair(held, other, me, bit).reshape((-1,) + series.shape)
    held_d, held_s = outs[0]
    for idx, bit in enumerate(order):
        other_d, other_s = outs[idx + 1]
        held_d = place_pair(held_d, other_d, me, bit).reshape((-1, row_count, seeds))
        held_s = place_pair(held_s, other_s, me, bit).reshape((-1, row_count, seeds))
    out_block = jnp.zeros((row_count, seeds), jnp.bfloat16)
    dispersion = unpermute(held_d.reshape((2,) * bits + (row_count, seeds)), order, size, out_block)
    statistic = unpermute(held_s.reshape((2,) * bits + (row_count, seeds)), order, size, out_block)
    return (dispersion.reshape(size, row_count, seeds), statistic.reshape(size, row_count, seeds))


def solution(mesh):
    from jax.sharding import Mesh
    split = Mesh(mesh.devices.reshape(2, 4, 2, 2, 16), BLK_AXES + WIDE_AXES)
    every = BLK_AXES + WIDE_AXES
    in_specs = (P(every, None), P(), P(every))
    out_specs = (P(None, WIDE_AXES, BLK_AXES), P(None, WIDE_AXES, BLK_AXES))
    return jax.shard_map(body, mesh=split, in_specs=in_specs, out_specs=out_specs, check_vma=False)
```

```python
import numpy as np
import jax
import jax.numpy as jnp
from jax import lax
from jax.experimental import pallas as pl
from jax.experimental.pallas import tpu as pltpu
from jax.sharding import PartitionSpec as P

WIN = 60
STRIDE = 30
NWIN = 20
LANES = 128
SPAN = 256
ROW_TILE = 16
NT = (((1,), (1,)), ((), ()))


EPSILON = 1e-05
CLIP_LEVEL = 0.99


def fisher_of(values):
    clipped = jnp.clip(values, -CLIP_LEVEL, CLIP_LEVEL)
    return 0.5 * (jnp.log(1.0 + clipped) - jnp.log(1.0 - clipped))


def window_frames(frames):
    out = []
    for n in range(NWIN):
        start = LANES * ((STRIDE * n) // LANES)
        width = LANES if STRIDE * n - start + WIN <= LANES else SPAN
        out.append((start, min(width, frames - start)))
    return out


def prepare(raw_rows, scrub_mask):
    values = raw_rows.astype(jnp.float32)
    row_count = values.shape[0]
    weight = scrub_mask.astype(jnp.float32)
    covered = STRIDE * (NWIN + 1)
    pieces = values[:, :covered].reshape(row_count, NWIN + 1, STRIDE)
    framed = jnp.concatenate([pieces[:, :-1], pieces[:, 1:]], axis=2)
    mask_pieces = weight[:covered].reshape(NWIN + 1, STRIDE)
    mask_framed = jnp.concatenate([mask_pieces[:-1], mask_pieces[1:]], axis=1)
    valid_count = jnp.sum(mask_framed, axis=1)
    centre = jnp.sum(framed * mask_framed, axis=2) / valid_count
    centred = (framed - centre[:, :, None]) * mask_framed
    spread = jnp.sum(centred * centred, axis=2)
    windows = (centred * lax.rsqrt(spread + EPSILON)[:, :, None]).astype(jnp.bfloat16)
    total_valid = jnp.sum(weight)
    mean_all = jnp.sum(values * weight, axis=1) / total_valid
    centred_all = (values - mean_all[:, None]) * weight
    spread_all = jnp.sum(centred_all * centred_all, axis=1)
    whole_std = (centred_all * lax.rsqrt(spread_all + EPSILON)[:, None]).astype(jnp.bfloat16)
    return (windows, whole_std)


def seed_operands(seed_window, seed_whole, frames):
    blocks = []
    for n, (start, width) in enumerate(window_frames(frames)):
        left = STRIDE * n - start
        part = seed_window[:, n, :]
        part = jnp.pad(part, ((0, 0), (left, SPAN - WIN - left)))
        blocks.append(part.T)
    return jnp.stack(blocks), seed_whole.T


def window_masks(weight, frames):
    padded = jnp.pad(weight, (0, SPAN))
    rows = []
    for n, (start, width) in enumerate(window_frames(frames)):
        local = np.arange(SPAN) + start
        inside = (local >= STRIDE * n) & (local < STRIDE * n + WIN)
        rows.append(padded[start:start + SPAN] * inside.astype(np.float32))
    return jnp.stack(rows)


def fisher_ratio(values):
    clipped = jnp.clip(values, -CLIP_LEVEL, CLIP_LEVEL)
    return 0.5 * jnp.log((1.0 + clipped) / (1.0 - clipped))


def compare_kernel(x_ref, m_ref, mw_ref, sw_ref, sh_ref, disp_ref, stat_ref):
    frames = x_ref.shape[1]
    x = x_ref[...].astype(jnp.float32)
    m = m_ref[...]
    total_valid = jnp.sum(m)
    mean_all = jnp.sum(x * m, axis=1, keepdims=True) / total_valid
    centred = (x - mean_all) * m
    spread = jnp.sum(centred * centred, axis=1, keepdims=True)
    whole = (centred * lax.rsqrt(spread + EPSILON)).astype(jnp.bfloat16)
    q = lax.dot_general(whole, sh_ref[...], NT, preferred_element_type=jnp.float32)
    stat_ref[...] = (jnp.sqrt(total_valid - 3.0) * fisher_of(q)).astype(stat_ref.dtype)
    first = None
    second = None
    for n, (start, width) in enumerate(window_frames(frames)):
        xw = x[:, start:start + width]
        mw = mw_ref[n:n + 1, :width]
        count = jnp.sum(mw)
        centre = jnp.sum(xw * mw, axis=1, keepdims=True) / count
        cw = (xw - centre) * mw
        sp = jnp.sum(cw * cw, axis=1, keepdims=True)
        w = (cw * lax.rsqrt(sp + EPSILON)).astype(jnp.bfloat16)
        r = lax.dot_general(w, sw_ref[n, :, :width], NT, preferred_element_type=jnp.float32)
        z = fisher_ratio(r)
        if first is None:
            first, second = z, z * z
        else:
            first, second = first + z, second + z * z
    first = first / NWIN
    second = second / NWIN
    disp_ref[...] = ((WIN - 3) * (second - first * first)).astype(disp_ref.dtype)


def seed_kernel(x_ref, m_ref, mw_ref, sw_ref, sh_ref):
    frames = x_ref.shape[1]
    x = x_ref[...].astype(jnp.float32)
    m = m_ref[...]
    total_valid = jnp.sum(m)
    mean_all = jnp.sum(x * m, axis=1, keepdims=True) / total_valid
    centred = (x - mean_all) * m
    spread = jnp.sum(centred * centred, axis=1, keepdims=True)
    sh_ref[...] = (centred * lax.rsqrt(spread + EPSILON)).astype(sh_ref.dtype)
    for n, (start, width) in enumerate(window_frames(frames)):
        xw = x[:, start:start + width]
        mw = mw_ref[n:n + 1, :width]
        count = jnp.sum(mw)
        centre = jnp.sum(xw * mw, axis=1, keepdims=True) / count
        cw = (xw - centre) * mw
        sp = jnp.sum(cw * cw, axis=1, keepdims=True)
        sw_ref[n, :, :width] = (cw * lax.rsqrt(sp + EPSILON)).astype(sw_ref.dtype)
        if width < SPAN:
            sw_ref[n, :, width:] = jnp.zeros((x.shape[0], SPAN - width), sw_ref.dtype)


def seed_rows(rows, m, mw):
    seeds, frames = rows.shape
    vmem = pl.BlockSpec(memory_space=pltpu.VMEM)
    return pl.pallas_call(
        seed_kernel,
        in_specs=[vmem, vmem, vmem],
        out_specs=[vmem, vmem],
        out_shape=[
            jax.ShapeDtypeStruct((NWIN, seeds, SPAN), jnp.bfloat16),
            jax.ShapeDtypeStruct((seeds, frames), jnp.bfloat16),
        ],
    )(rows, m, mw)


def compare_rows(rows, m, mw, sw, sh, block):
    count, frames = rows.shape
    seeds = sh.shape[0]
    steps = count // block
    cost = pl.CostEstimate(
        flops=2 * count * seeds * (frames + NWIN * SPAN),
        transcendentals=2 * count * seeds * (NWIN + 1),
        bytes_accessed=count * frames * 2 + sw.size * 2 + 2 * count * seeds * 2,
    )
    out = jax.ShapeDtypeStruct((count, seeds), jnp.bfloat16)
    return pl.pallas_call(
        compare_kernel,
        grid=(steps,),
        in_specs=[
            pl.BlockSpec((block, frames), lambda i: (i, 0)),
            pl.BlockSpec((1, frames), lambda i: (0, 0)),
            pl.BlockSpec((NWIN, SPAN), lambda i: (0, 0)),
            pl.BlockSpec((NWIN, seeds, SPAN), lambda i: (0, 0, 0)),
            pl.BlockSpec((seeds, frames), lambda i: (0, 0)),
        ],
        out_specs=[
            pl.BlockSpec((block, seeds), lambda i: (i, 0)),
            pl.BlockSpec((block, seeds), lambda i: (i, 0)),
        ],
        out_shape=[out, out],
        cost_estimate=cost,
        compiler_params=pltpu.CompilerParams(vmem_limit_bytes=48 * 1024 * 1024),
    )(rows, m, mw, sw, sh)


def doubling_gather(block, axis):
    size = lax.axis_size(axis)
    me = lax.axis_index(axis)
    bits = size.bit_length() - 1
    low = list(range(bits - 1))[::-1]
    order = low + [bits - 1] if bits > 1 else [0]
    held = block[None]
    for bit in order:
        stride = 1 << bit
        route = [(i, i ^ stride) for i in range(size)]
        other = lax.ppermute(held, axis, route)
        held = place_pair(held, other, me, bit)
    return unpermute(held, order, size, block)


def place_pair(held, other, me, bit):
    mine_low = ((me >> bit) & 1) == 0
    return jnp.where(mine_low, jnp.stack([held, other]), jnp.stack([other, held]))


def unpermute(held, order, size, block):
    bits = len(order)
    placed = order[::-1]
    perm = [placed.index(bits - 1 - j) for j in range(bits)]
    held = held.reshape((2,) * bits + block.shape)
    held = jnp.transpose(held, perm + [bits + k for k in range(block.ndim)])
    return held.reshape((size * block.shape[0],) + block.shape[1:])


BLK_AXES = ("x_hi", "y", "core")
WIDE_AXES = ("x_lo", "z")


def body(series, scrub_mask, seed_index):
    row_count, frames = series.shape
    local_rows = seed_index % row_count
    own_seeds = jnp.take(series, local_rows, axis=0)
    weight = scrub_mask.astype(jnp.float32)
    panel_rows = lax.all_gather(own_seeds, "z", axis=0, tiled=True)
    panel_rows = lax.all_gather(panel_rows, "x_lo", axis=0, tiled=True)
    mw = window_masks(weight, frames)
    m = weight[None, :]
    sw, sh = seed_rows(panel_rows, m, mw)
    seeds = panel_rows.shape[0]
    size = 1
    for a in BLK_AXES:
        size *= lax.axis_size(a)
    me = lax.axis_index(BLK_AXES)
    bits = size.bit_length() - 1
    order = list(range(bits))[::-1]

    def run(rows):
        count = rows.shape[0] * rows.shape[1]
        d, s = compare_rows(rows.reshape(count, frames), m, mw, sw, sh, row_count)
        return d.reshape(rows.shape[0], row_count, seeds), s.reshape(rows.shape[0], row_count, seeds)

    held = series[None]
    outs = [run(held)]
    for idx, bit in enumerate(order):
        stride = 1 << bit
        route = [(i, i ^ stride) for i in range(size)]
        if idx > 0:
            held, prev_d, prev_s = lax.optimization_barrier((held,) + outs[idx - 1])
            outs[idx - 1] = (prev_d, prev_s)
        other = lax.ppermute(held, BLK_AXES, route)
        outs.append(run(other))
        held = place_pair(held, other, me, bit).reshape((-1,) + series.shape)
    held_d, held_s = outs[0]
    for idx, bit in enumerate(order):
        other_d, other_s = outs[idx + 1]
        held_d = place_pair(held_d, other_d, me, bit).reshape((-1, row_count, seeds))
        held_s = place_pair(held_s, other_s, me, bit).reshape((-1, row_count, seeds))
    out_block = jnp.zeros((row_count, seeds), jnp.bfloat16)
    dispersion = unpermute(held_d.reshape((2,) * bits + (row_count, seeds)), order, size, out_block)
    statistic = unpermute(held_s.reshape((2,) * bits + (row_count, seeds)), order, size, out_block)
    return (dispersion.reshape(size, row_count, seeds), statistic.reshape(size, row_count, seeds))


def solution(mesh):
    from jax.sharding import Mesh
    split = Mesh(mesh.devices.reshape(2, 4, 2, 2, 16), BLK_AXES + WIDE_AXES)
    every = BLK_AXES + WIDE_AXES
    in_specs = (P(every, None), P(), P(every))
    out_specs = (P(None, WIDE_AXES, BLK_AXES), P(None, WIDE_AXES, BLK_AXES))
    return jax.shard_map(body, mesh=split, in_specs=in_specs, out_specs=out_specs, check_vma=False)
```

```python
import numpy as np
import jax
import jax.numpy as jnp
from jax import lax
from jax.experimental import pallas as pl
from jax.experimental.pallas import tpu as pltpu
from jax.sharding import PartitionSpec as P

WIN = 60
STRIDE = 30
NWIN = 20
LANES = 128
SPAN = 256
ROW_TILE = 16
NT = (((1,), (1,)), ((), ()))
HALF_LN2 = 0.5 * float(np.log(2.0))


EPSILON = 1e-05
CLIP_LEVEL = 0.99


def fisher_of(values):
    clipped = jnp.clip(values, -CLIP_LEVEL, CLIP_LEVEL)
    return 0.5 * (jnp.log(1.0 + clipped) - jnp.log(1.0 - clipped))


def window_frames(frames):
    out = []
    for n in range(NWIN):
        start = LANES * ((STRIDE * n) // LANES)
        width = LANES if STRIDE * n - start + WIN <= LANES else SPAN
        out.append((start, min(width, frames - start)))
    return out


def prepare(raw_rows, scrub_mask):
    values = raw_rows.astype(jnp.float32)
    row_count = values.shape[0]
    weight = scrub_mask.astype(jnp.float32)
    covered = STRIDE * (NWIN + 1)
    pieces = values[:, :covered].reshape(row_count, NWIN + 1, STRIDE)
    framed = jnp.concatenate([pieces[:, :-1], pieces[:, 1:]], axis=2)
    mask_pieces = weight[:covered].reshape(NWIN + 1, STRIDE)
    mask_framed = jnp.concatenate([mask_pieces[:-1], mask_pieces[1:]], axis=1)
    valid_count = jnp.sum(mask_framed, axis=1)
    centre = jnp.sum(framed * mask_framed, axis=2) / valid_count
    centred = (framed - centre[:, :, None]) * mask_framed
    spread = jnp.sum(centred * centred, axis=2)
    windows = (centred * lax.rsqrt(spread + EPSILON)[:, :, None]).astype(jnp.bfloat16)
    total_valid = jnp.sum(weight)
    mean_all = jnp.sum(values * weight, axis=1) / total_valid
    centred_all = (values - mean_all[:, None]) * weight
    spread_all = jnp.sum(centred_all * centred_all, axis=1)
    whole_std = (centred_all * lax.rsqrt(spread_all + EPSILON)[:, None]).astype(jnp.bfloat16)
    return (windows, whole_std)


def seed_operands(seed_window, seed_whole, frames):
    blocks = []
    for n, (start, width) in enumerate(window_frames(frames)):
        left = STRIDE * n - start
        part = seed_window[:, n, :]
        part = jnp.pad(part, ((0, 0), (left, SPAN - WIN - left)))
        blocks.append(part.T)
    return jnp.stack(blocks), seed_whole.T


def window_masks(weight, frames):
    padded = jnp.pad(weight, (0, SPAN))
    rows = []
    for n, (start, width) in enumerate(window_frames(frames)):
        local = np.arange(SPAN) + start
        inside = (local >= STRIDE * n) & (local < STRIDE * n + WIN)
        rows.append(padded[start:start + SPAN] * inside.astype(np.float32))
    return jnp.stack(rows)


def compare_kernel(x_ref, m_ref, mw_ref, sw_ref, sh_ref, disp_ref, stat_ref):
    frames = x_ref.shape[1]
    x = x_ref[...].astype(jnp.float32)
    m = m_ref[...]
    total_valid = jnp.sum(m)
    mean_all = jnp.sum(x * m, axis=1, keepdims=True) / total_valid
    centred = (x - mean_all) * m
    spread = jnp.sum(centred * centred, axis=1, keepdims=True)
    whole = (centred * lax.rsqrt(spread + EPSILON)).astype(jnp.bfloat16)
    q = lax.dot_general(whole, sh_ref[...], NT, preferred_element_type=jnp.float32)
    stat_ref[...] = (jnp.sqrt(total_valid - 3.0) * fisher_of(q)).astype(stat_ref.dtype)
    first = None
    second = None
    for n, (start, width) in enumerate(window_frames(frames)):
        xw = x[:, start:start + width]
        mw = mw_ref[n:n + 1, :width]
        count = jnp.sum(mw)
        centre = jnp.sum(xw * mw, axis=1, keepdims=True) / count
        cw = (xw - centre) * mw
        sp = jnp.sum(cw * cw, axis=1, keepdims=True)
        w = (cw * lax.rsqrt(sp + EPSILON)).astype(jnp.bfloat16)
        r = lax.dot_general(w, sw_ref[n, :, :width], NT, preferred_element_type=jnp.float32)
        clipped = jnp.clip(r, -CLIP_LEVEL, CLIP_LEVEL)
        z2 = lax.log2(1.0 + clipped) - lax.log2(1.0 - clipped)
        if first is None:
            first, second = z2, z2 * z2
        else:
            first, second = first + z2, second + z2 * z2
    first = first * (HALF_LN2 / NWIN)
    second = second * (HALF_LN2 * HALF_LN2 / NWIN)
    disp_ref[...] = ((WIN - 3) * (second - first * first)).astype(disp_ref.dtype)


def seed_kernel(x_ref, m_ref, mw_ref, sw_ref, sh_ref):
    frames = x_ref.shape[1]
    x = x_ref[...].astype(jnp.float32)
    m = m_ref[...]
    total_valid = jnp.sum(m)
    mean_all = jnp.sum(x * m, axis=1, keepdims=True) / total_valid
    centred = (x - mean_all) * m
    spread = jnp.sum(centred * centred, axis=1, keepdims=True)
    sh_ref[...] = (centred * lax.rsqrt(spread + EPSILON)).astype(sh_ref.dtype)
    for n, (start, width) in enumerate(window_frames(frames)):
        xw = x[:, start:start + width]
        mw = mw_ref[n:n + 1, :width]
        count = jnp.sum(mw)
        centre = jnp.sum(xw * mw, axis=1, keepdims=True) / count
        cw = (xw - centre) * mw
        sp = jnp.sum(cw * cw, axis=1, keepdims=True)
        sw_ref[n, :, :width] = (cw * lax.rsqrt(sp + EPSILON)).astype(sw_ref.dtype)
        if width < SPAN:
            sw_ref[n, :, width:] = jnp.zeros((x.shape[0], SPAN - width), sw_ref.dtype)


def seed_rows(rows, m, mw):
    seeds, frames = rows.shape
    vmem = pl.BlockSpec(memory_space=pltpu.VMEM)
    return pl.pallas_call(
        seed_kernel,
        in_specs=[vmem, vmem, vmem],
        out_specs=[vmem, vmem],
        out_shape=[
            jax.ShapeDtypeStruct((NWIN, seeds, SPAN), jnp.bfloat16),
            jax.ShapeDtypeStruct((seeds, frames), jnp.bfloat16),
        ],
    )(rows, m, mw)


def compare_rows(rows, m, mw, sw, sh, block):
    count, frames = rows.shape
    seeds = sh.shape[0]
    steps = count // block
    cost = pl.CostEstimate(
        flops=2 * count * seeds * (frames + NWIN * SPAN),
        transcendentals=2 * count * seeds * (NWIN + 1),
        bytes_accessed=count * frames * 2 + sw.size * 2 + 2 * count * seeds * 2,
    )
    out = jax.ShapeDtypeStruct((count, seeds), jnp.bfloat16)
    return pl.pallas_call(
        compare_kernel,
        grid=(steps,),
        in_specs=[
            pl.BlockSpec((block, frames), lambda i: (i, 0)),
            pl.BlockSpec((1, frames), lambda i: (0, 0)),
            pl.BlockSpec((NWIN, SPAN), lambda i: (0, 0)),
            pl.BlockSpec((NWIN, seeds, SPAN), lambda i: (0, 0, 0)),
            pl.BlockSpec((seeds, frames), lambda i: (0, 0)),
        ],
        out_specs=[
            pl.BlockSpec((block, seeds), lambda i: (i, 0)),
            pl.BlockSpec((block, seeds), lambda i: (i, 0)),
        ],
        out_shape=[out, out],
        cost_estimate=cost,
        compiler_params=pltpu.CompilerParams(vmem_limit_bytes=48 * 1024 * 1024),
    )(rows, m, mw, sw, sh)


def doubling_gather(block, axis):
    size = lax.axis_size(axis)
    me = lax.axis_index(axis)
    bits = size.bit_length() - 1
    low = list(range(bits - 1))[::-1]
    order = low + [bits - 1] if bits > 1 else [0]
    held = block[None]
    for bit in order:
        stride = 1 << bit
        route = [(i, i ^ stride) for i in range(size)]
        other = lax.ppermute(held, axis, route)
        held = place_pair(held, other, me, bit)
    return unpermute(held, order, size, block)


def place_pair(held, other, me, bit):
    mine_low = ((me >> bit) & 1) == 0
    return jnp.where(mine_low, jnp.stack([held, other]), jnp.stack([other, held]))


def unpermute(held, order, size, block):
    bits = len(order)
    placed = order[::-1]
    perm = [placed.index(bits - 1 - j) for j in range(bits)]
    held = held.reshape((2,) * bits + block.shape)
    held = jnp.transpose(held, perm + [bits + k for k in range(block.ndim)])
    return held.reshape((size * block.shape[0],) + block.shape[1:])


BLK_AXES = ("x_hi", "y", "core")
WIDE_AXES = ("x_lo", "z")


def body(series, scrub_mask, seed_index):
    row_count, frames = series.shape
    local_rows = seed_index % row_count
    own_seeds = jnp.take(series, local_rows, axis=0)
    weight = scrub_mask.astype(jnp.float32)
    panel_rows = lax.all_gather(own_seeds, "z", axis=0, tiled=True)
    panel_rows = lax.all_gather(panel_rows, "x_lo", axis=0, tiled=True)
    mw = window_masks(weight, frames)
    m = weight[None, :]
    sw, sh = seed_rows(panel_rows, m, mw)
    seeds = panel_rows.shape[0]
    size = 1
    for a in BLK_AXES:
        size *= lax.axis_size(a)
    me = lax.axis_index(BLK_AXES)
    bits = size.bit_length() - 1
    order = list(range(bits))[::-1]

    def run(rows):
        count = rows.shape[0] * rows.shape[1]
        d, s = compare_rows(rows.reshape(count, frames), m, mw, sw, sh, row_count)
        return d.reshape(rows.shape[0], row_count, seeds), s.reshape(rows.shape[0], row_count, seeds)

    held = series[None]
    outs = [run(held)]
    for idx, bit in enumerate(order):
        stride = 1 << bit
        route = [(i, i ^ stride) for i in range(size)]
        if idx > 0:
            held, prev_d, prev_s = lax.optimization_barrier((held,) + outs[idx - 1])
            outs[idx - 1] = (prev_d, prev_s)
        other = lax.ppermute(held, BLK_AXES, route)
        outs.append(run(other))
        held = place_pair(held, other, me, bit).reshape((-1,) + series.shape)
    held_d, held_s = outs[0]
    for idx, bit in enumerate(order):
        other_d, other_s = outs[idx + 1]
        held_d = place_pair(held_d, other_d, me, bit).reshape((-1, row_count, seeds))
        held_s = place_pair(held_s, other_s, me, bit).reshape((-1, row_count, seeds))
    out_block = jnp.zeros((row_count, seeds), jnp.bfloat16)
    dispersion = unpermute(held_d.reshape((2,) * bits + (row_count, seeds)), order, size, out_block)
    statistic = unpermute(held_s.reshape((2,) * bits + (row_count, seeds)), order, size, out_block)
    return (dispersion.reshape(size, row_count, seeds), statistic.reshape(size, row_count, seeds))


def solution(mesh):
    from jax.sharding import Mesh
    split = Mesh(mesh.devices.reshape(2, 4, 2, 2, 16), BLK_AXES + WIDE_AXES)
    every = BLK_AXES + WIDE_AXES
    in_specs = (P(every, None), P(), P(every))
    out_specs = (P(None, WIDE_AXES, BLK_AXES), P(None, WIDE_AXES, BLK_AXES))
    return jax.shard_map(body, mesh=split, in_specs=in_specs, out_specs=out_specs, check_vma=False)
```

```python
import numpy as np
import jax
import jax.numpy as jnp
from jax import lax
from jax.experimental import pallas as pl
from jax.experimental.pallas import tpu as pltpu
from jax.sharding import PartitionSpec as P

WIN = 60
STRIDE = 30
NWIN = 20
LANES = 128
SPAN = 256
ROW_TILE = 16
NT = (((1,), (1,)), ((), ()))
HALF_LN2 = 0.5 * float(np.log(2.0))


EPSILON = 1e-05
CLIP_LEVEL = 0.99


def fisher_of(values):
    clipped = jnp.clip(values, -CLIP_LEVEL, CLIP_LEVEL)
    return 0.5 * (jnp.log(1.0 + clipped) - jnp.log(1.0 - clipped))


def window_frames(frames):
    out = []
    for n in range(NWIN):
        start = LANES * ((STRIDE * n) // LANES)
        width = LANES if STRIDE * n - start + WIN <= LANES else SPAN
        out.append((start, min(width, frames - start)))
    return out


def prepare(raw_rows, scrub_mask):
    values = raw_rows.astype(jnp.float32)
    row_count = values.shape[0]
    weight = scrub_mask.astype(jnp.float32)
    covered = STRIDE * (NWIN + 1)
    pieces = values[:, :covered].reshape(row_count, NWIN + 1, STRIDE)
    framed = jnp.concatenate([pieces[:, :-1], pieces[:, 1:]], axis=2)
    mask_pieces = weight[:covered].reshape(NWIN + 1, STRIDE)
    mask_framed = jnp.concatenate([mask_pieces[:-1], mask_pieces[1:]], axis=1)
    valid_count = jnp.sum(mask_framed, axis=1)
    centre = jnp.sum(framed * mask_framed, axis=2) / valid_count
    centred = (framed - centre[:, :, None]) * mask_framed
    spread = jnp.sum(centred * centred, axis=2)
    windows = (centred * lax.rsqrt(spread + EPSILON)[:, :, None]).astype(jnp.bfloat16)
    total_valid = jnp.sum(weight)
    mean_all = jnp.sum(values * weight, axis=1) / total_valid
    centred_all = (values - mean_all[:, None]) * weight
    spread_all = jnp.sum(centred_all * centred_all, axis=1)
    whole_std = (centred_all * lax.rsqrt(spread_all + EPSILON)[:, None]).astype(jnp.bfloat16)
    return (windows, whole_std)


def seed_operands(seed_window, seed_whole, frames):
    blocks = []
    for n, (start, width) in enumerate(window_frames(frames)):
        left = STRIDE * n - start
        part = seed_window[:, n, :]
        part = jnp.pad(part, ((0, 0), (left, SPAN - WIN - left)))
        blocks.append(part.T)
    return jnp.stack(blocks), seed_whole.T


def window_masks(weight, frames):
    padded = jnp.pad(weight, (0, SPAN))
    rows = []
    for n, (start, width) in enumerate(window_frames(frames)):
        local = np.arange(SPAN) + start
        inside = (local >= STRIDE * n) & (local < STRIDE * n + WIN)
        rows.append(padded[start:start + SPAN] * inside.astype(np.float32))
    return jnp.stack(rows)


def compare_kernel(x_ref, m_ref, mw_ref, sw_ref, sh_ref, disp_ref, stat_ref):
    frames = x_ref.shape[1]
    x = x_ref[...].astype(jnp.float32)
    m = m_ref[...]
    total_valid = jnp.sum(m)
    mean_all = jnp.sum(x * m, axis=1, keepdims=True) / total_valid
    centred = (x - mean_all) * m
    spread = jnp.sum(centred * centred, axis=1, keepdims=True)
    whole = (centred * lax.rsqrt(spread + EPSILON)).astype(jnp.bfloat16)
    q = lax.dot_general(whole, sh_ref[...], NT, preferred_element_type=jnp.float32)
    stat_ref[...] = (jnp.sqrt(total_valid - 3.0) * fisher_of(q)).astype(stat_ref.dtype)
    first = None
    second = None
    for n, (start, width) in enumerate(window_frames(frames)):
        xw = x[:, start:start + width]
        mw = mw_ref[n:n + 1, :width]
        count = jnp.sum(mw)
        centre = jnp.sum(xw * mw, axis=1, keepdims=True) / count
        cw = (xw - centre) * mw
        sp = jnp.sum(cw * cw, axis=1, keepdims=True)
        w = (cw * lax.rsqrt(sp + EPSILON)).astype(jnp.bfloat16)
        r = lax.dot_general(w, sw_ref[n, :, :width], NT, preferred_element_type=jnp.float32)
        clipped = jnp.clip(r, -CLIP_LEVEL, CLIP_LEVEL)
        z2 = lax.log2(1.0 + clipped) - lax.log2(1.0 - clipped)
        if first is None:
            first, second = z2, z2 * z2
        else:
            first, second = first + z2, second + z2 * z2
    first = first * (HALF_LN2 / NWIN)
    second = second * (HALF_LN2 * HALF_LN2 / NWIN)
    disp_ref[...] = ((WIN - 3) * (second - first * first)).astype(disp_ref.dtype)


def seed_kernel(x_ref, m_ref, mw_ref, sw_ref, sh_ref):
    frames = x_ref.shape[1]
    x = x_ref[...].astype(jnp.float32)
    m = m_ref[...]
    total_valid = jnp.sum(m)
    mean_all = jnp.sum(x * m, axis=1, keepdims=True) / total_valid
    centred = (x - mean_all) * m
    spread = jnp.sum(centred * centred, axis=1, keepdims=True)
    sh_ref[...] = (centred * lax.rsqrt(spread + EPSILON)).astype(sh_ref.dtype)
    for n, (start, width) in enumerate(window_frames(frames)):
        xw = x[:, start:start + width]
        mw = mw_ref[n:n + 1, :width]
        count = jnp.sum(mw)
        centre = jnp.sum(xw * mw, axis=1, keepdims=True) / count
        cw = (xw - centre) * mw
        sp = jnp.sum(cw * cw, axis=1, keepdims=True)
        sw_ref[n, :, :width] = (cw * lax.rsqrt(sp + EPSILON)).astype(sw_ref.dtype)
        if width < SPAN:
            sw_ref[n, :, width:] = jnp.zeros((x.shape[0], SPAN - width), sw_ref.dtype)


def seed_rows(rows, m, mw):
    seeds, frames = rows.shape
    vmem = pl.BlockSpec(memory_space=pltpu.VMEM)
    return pl.pallas_call(
        seed_kernel,
        in_specs=[vmem, vmem, vmem],
        out_specs=[vmem, vmem],
        out_shape=[
            jax.ShapeDtypeStruct((NWIN, seeds, SPAN), jnp.bfloat16),
            jax.ShapeDtypeStruct((seeds, frames), jnp.bfloat16),
        ],
    )(rows, m, mw)


def compare_rows(rows, m, mw, sw, sh, block):
    count, frames = rows.shape
    seeds = sh.shape[0]
    steps = count // block
    cost = pl.CostEstimate(
        flops=2 * count * seeds * (frames + NWIN * SPAN),
        transcendentals=2 * count * seeds * (NWIN + 1),
        bytes_accessed=count * frames * 2 + sw.size * 2 + 2 * count * seeds * 2,
    )
    out = jax.ShapeDtypeStruct((count, seeds), jnp.bfloat16)
    return pl.pallas_call(
        compare_kernel,
        grid=(steps,),
        in_specs=[
            pl.BlockSpec((block, frames), lambda i: (i, 0)),
            pl.BlockSpec((1, frames), lambda i: (0, 0)),
            pl.BlockSpec((NWIN, SPAN), lambda i: (0, 0)),
            pl.BlockSpec((NWIN, seeds, SPAN), lambda i: (0, 0, 0)),
            pl.BlockSpec((seeds, frames), lambda i: (0, 0)),
        ],
        out_specs=[
            pl.BlockSpec((block, seeds), lambda i: (i, 0)),
            pl.BlockSpec((block, seeds), lambda i: (i, 0)),
        ],
        out_shape=[out, out],
        cost_estimate=cost,
        compiler_params=pltpu.CompilerParams(vmem_limit_bytes=48 * 1024 * 1024),
    )(rows, m, mw, sw, sh)


def doubling_gather(block, axis):
    size = lax.axis_size(axis)
    me = lax.axis_index(axis)
    bits = size.bit_length() - 1
    low = list(range(bits - 1))[::-1]
    order = low + [bits - 1] if bits > 1 else [0]
    held = block[None]
    for bit in order:
        stride = 1 << bit
        route = [(i, i ^ stride) for i in range(size)]
        other = lax.ppermute(held, axis, route)
        held = place_pair(held, other, me, bit)
    return unpermute(held, order, size, block)


def place_pair(held, other, me, bit):
    mine_low = ((me >> bit) & 1) == 0
    return jnp.where(mine_low, jnp.stack([held, other]), jnp.stack([other, held]))


def unpermute(held, order, size, block):
    bits = len(order)
    placed = order[::-1]
    perm = [placed.index(bits - 1 - j) for j in range(bits)]
    held = held.reshape((2,) * bits + block.shape)
    held = jnp.transpose(held, perm + [bits + k for k in range(block.ndim)])
    return held.reshape((size * block.shape[0],) + block.shape[1:])


BLK_AXES = ("x_hi", "y", "core")
WIDE_AXES = ("x_lo", "z")


def body(series, scrub_mask, seed_index):
    row_count, frames = series.shape
    local_rows = seed_index % row_count
    own_seeds = jnp.take(series, local_rows, axis=0)
    weight = scrub_mask.astype(jnp.float32)
    gathered = lax.all_gather(series, BLK_AXES, axis=0, tiled=True)
    panel_rows = lax.all_gather(own_seeds, "z", axis=0, tiled=True)
    panel_rows = lax.all_gather(panel_rows, "x_lo", axis=0, tiled=True)
    mw = window_masks(weight, frames)
    m = weight[None, :]
    sw, sh = seed_rows(panel_rows, m, mw)
    seeds = panel_rows.shape[0]
    blocks = 1
    for a in BLK_AXES:
        blocks *= lax.axis_size(a)
    dispersion, statistic = compare_rows(gathered, m, mw, sw, sh, row_count)
    shape = (blocks, row_count, seeds)
    return (dispersion.reshape(shape), statistic.reshape(shape))


def solution(mesh):
    from jax.sharding import Mesh
    split = Mesh(mesh.devices.reshape(2, 4, 2, 2, 16), BLK_AXES + WIDE_AXES)
    every = BLK_AXES + WIDE_AXES
    in_specs = (P(every, None), P(), P(every))
    out_specs = (P(None, WIDE_AXES, BLK_AXES), P(None, WIDE_AXES, BLK_AXES))
    return jax.shard_map(body, mesh=split, in_specs=in_specs, out_specs=out_specs, check_vma=False)
```

```python
import numpy as np
import jax
import jax.numpy as jnp
from jax import lax
from jax.experimental import pallas as pl
from jax.experimental.pallas import tpu as pltpu
from jax.sharding import PartitionSpec as P

WIN = 60
STRIDE = 30
NWIN = 20
LANES = 128
SPAN = 256
ROW_TILE = 16
NT = (((1,), (1,)), ((), ()))
HALF_LN2 = 0.5 * float(np.log(2.0))


EPSILON = 1e-05
CLIP_LEVEL = 0.99


def fisher_of(values):
    clipped = jnp.clip(values, -CLIP_LEVEL, CLIP_LEVEL)
    return 0.5 * (jnp.log(1.0 + clipped) - jnp.log(1.0 - clipped))


def window_frames(frames):
    out = []
    for n in range(NWIN):
        start = LANES * ((STRIDE * n) // LANES)
        width = LANES if STRIDE * n - start + WIN <= LANES else SPAN
        out.append((start, min(width, frames - start)))
    return out


def prepare(raw_rows, scrub_mask):
    values = raw_rows.astype(jnp.float32)
    row_count = values.shape[0]
    weight = scrub_mask.astype(jnp.float32)
    covered = STRIDE * (NWIN + 1)
    pieces = values[:, :covered].reshape(row_count, NWIN + 1, STRIDE)
    framed = jnp.concatenate([pieces[:, :-1], pieces[:, 1:]], axis=2)
    mask_pieces = weight[:covered].reshape(NWIN + 1, STRIDE)
    mask_framed = jnp.concatenate([mask_pieces[:-1], mask_pieces[1:]], axis=1)
    valid_count = jnp.sum(mask_framed, axis=1)
    centre = jnp.sum(framed * mask_framed, axis=2) / valid_count
    centred = (framed - centre[:, :, None]) * mask_framed
    spread = jnp.sum(centred * centred, axis=2)
    windows = (centred * lax.rsqrt(spread + EPSILON)[:, :, None]).astype(jnp.bfloat16)
    total_valid = jnp.sum(weight)
    mean_all = jnp.sum(values * weight, axis=1) / total_valid
    centred_all = (values - mean_all[:, None]) * weight
    spread_all = jnp.sum(centred_all * centred_all, axis=1)
    whole_std = (centred_all * lax.rsqrt(spread_all + EPSILON)[:, None]).astype(jnp.bfloat16)
    return (windows, whole_std)


def seed_operands(seed_window, seed_whole, frames):
    blocks = []
    for n, (start, width) in enumerate(window_frames(frames)):
        left = STRIDE * n - start
        part = seed_window[:, n, :]
        part = jnp.pad(part, ((0, 0), (left, SPAN - WIN - left)))
        blocks.append(part.T)
    return jnp.stack(blocks), seed_whole.T


def window_masks(weight, frames):
    padded = jnp.pad(weight, (0, SPAN))
    rows = []
    for n, (start, width) in enumerate(window_frames(frames)):
        local = np.arange(SPAN) + start
        inside = (local >= STRIDE * n) & (local < STRIDE * n + WIN)
        rows.append(padded[start:start + SPAN] * inside.astype(np.float32))
    return jnp.stack(rows)


def compare_kernel(x_ref, m_ref, mw_ref, sw_ref, sh_ref, disp_ref, stat_ref):
    frames = x_ref.shape[1]
    x = x_ref[...].astype(jnp.float32)
    m = m_ref[...]
    total_valid = jnp.sum(m)
    mean_all = jnp.sum(x * m, axis=1, keepdims=True) / total_valid
    centred = (x - mean_all) * m
    spread = jnp.sum(centred * centred, axis=1, keepdims=True)
    whole = (centred * lax.rsqrt(spread + EPSILON)).astype(jnp.bfloat16)
    q = lax.dot_general(whole, sh_ref[...], NT, preferred_element_type=jnp.float32)
    stat_ref[...] = (jnp.sqrt(total_valid - 3.0) * fisher_of(q)).astype(stat_ref.dtype)
    first = None
    second = None
    for n, (start, width) in enumerate(window_frames(frames)):
        xw = x[:, start:start + width]
        mw = mw_ref[n:n + 1, :width]
        count = jnp.sum(mw)
        centre = jnp.sum(xw * mw, axis=1, keepdims=True) / count
        cw = (xw - centre) * mw
        sp = jnp.sum(cw * cw, axis=1, keepdims=True)
        w = (cw * lax.rsqrt(sp + EPSILON)).astype(jnp.bfloat16)
        r = lax.dot_general(w, sw_ref[n, :, :width], NT, preferred_element_type=jnp.float32)
        clipped = jnp.clip(r, -CLIP_LEVEL, CLIP_LEVEL)
        z2 = lax.log2(1.0 + clipped) - lax.log2(1.0 - clipped)
        if first is None:
            first, second = z2, z2 * z2
        else:
            first, second = first + z2, second + z2 * z2
    first = first * (HALF_LN2 / NWIN)
    second = second * (HALF_LN2 * HALF_LN2 / NWIN)
    disp_ref[...] = ((WIN - 3) * (second - first * first)).astype(disp_ref.dtype)


def seed_kernel(x_ref, m_ref, mw_ref, sw_ref, sh_ref):
    frames = x_ref.shape[1]
    x = x_ref[...].astype(jnp.float32)
    m = m_ref[...]
    total_valid = jnp.sum(m)
    mean_all = jnp.sum(x * m, axis=1, keepdims=True) / total_valid
    centred = (x - mean_all) * m
    spread = jnp.sum(centred * centred, axis=1, keepdims=True)
    sh_ref[...] = (centred * lax.rsqrt(spread + EPSILON)).astype(sh_ref.dtype)
    for n, (start, width) in enumerate(window_frames(frames)):
        xw = x[:, start:start + width]
        mw = mw_ref[n:n + 1, :width]
        count = jnp.sum(mw)
        centre = jnp.sum(xw * mw, axis=1, keepdims=True) / count
        cw = (xw - centre) * mw
        sp = jnp.sum(cw * cw, axis=1, keepdims=True)
        sw_ref[n, :, :width] = (cw * lax.rsqrt(sp + EPSILON)).astype(sw_ref.dtype)
        if width < SPAN:
            sw_ref[n, :, width:] = jnp.zeros((x.shape[0], SPAN - width), sw_ref.dtype)


def seed_rows(rows, m, mw):
    seeds, frames = rows.shape
    vmem = pl.BlockSpec(memory_space=pltpu.VMEM)
    return pl.pallas_call(
        seed_kernel,
        in_specs=[vmem, vmem, vmem],
        out_specs=[vmem, vmem],
        out_shape=[
            jax.ShapeDtypeStruct((NWIN, seeds, SPAN), jnp.bfloat16),
            jax.ShapeDtypeStruct((seeds, frames), jnp.bfloat16),
        ],
    )(rows, m, mw)


def compare_rows(rows, m, mw, sw, sh, block):
    count, frames = rows.shape
    seeds = sh.shape[0]
    steps = count // block
    cost = pl.CostEstimate(
        flops=2 * count * seeds * (frames + NWIN * SPAN),
        transcendentals=2 * count * seeds * (NWIN + 1),
        bytes_accessed=count * frames * 2 + sw.size * 2 + 2 * count * seeds * 2,
    )
    out = jax.ShapeDtypeStruct((count, seeds), jnp.bfloat16)
    return pl.pallas_call(
        compare_kernel,
        grid=(steps,),
        in_specs=[
            pl.BlockSpec((block, frames), lambda i: (i, 0)),
            pl.BlockSpec((1, frames), lambda i: (0, 0)),
            pl.BlockSpec((NWIN, SPAN), lambda i: (0, 0)),
            pl.BlockSpec((NWIN, seeds, SPAN), lambda i: (0, 0, 0)),
            pl.BlockSpec((seeds, frames), lambda i: (0, 0)),
        ],
        out_specs=[
            pl.BlockSpec((block, seeds), lambda i: (i, 0)),
            pl.BlockSpec((block, seeds), lambda i: (i, 0)),
        ],
        out_shape=[out, out],
        cost_estimate=cost,
        compiler_params=pltpu.CompilerParams(vmem_limit_bytes=48 * 1024 * 1024),
    )(rows, m, mw, sw, sh)


def rest_kernel(p_ref, x_ref, m_ref, mw_ref, sw_ref, sh_ref, disp_ref, stat_ref):
    compare_kernel(x_ref, m_ref, mw_ref, sw_ref, sh_ref, disp_ref, stat_ref)


def compare_rest(rows, pair, m, mw, sw, sh, block, skip):
    count, frames = rows.shape
    seeds = sh.shape[0]
    steps = count // block - skip

    def pick(i, p):
        return jnp.where(i >= p[0], i + skip, i)

    cost = pl.CostEstimate(
        flops=2 * steps * block * seeds * (frames + NWIN * SPAN),
        transcendentals=2 * steps * block * seeds * (NWIN + 1),
        bytes_accessed=steps * block * (frames + 2 * seeds) * 2 + sw.size * 2,
    )
    out = jax.ShapeDtypeStruct((count, seeds), jnp.bfloat16)
    grid_spec = pltpu.PrefetchScalarGridSpec(
        num_scalar_prefetch=1,
        grid=(steps,),
        in_specs=[
            pl.BlockSpec((block, frames), lambda i, p: (pick(i, p), 0)),
            pl.BlockSpec((1, frames), lambda i, p: (0, 0)),
            pl.BlockSpec((NWIN, SPAN), lambda i, p: (0, 0)),
            pl.BlockSpec((NWIN, seeds, SPAN), lambda i, p: (0, 0, 0)),
            pl.BlockSpec((seeds, frames), lambda i, p: (0, 0)),
        ],
        out_specs=[
            pl.BlockSpec((block, seeds), lambda i, p: (pick(i, p), 0)),
            pl.BlockSpec((block, seeds), lambda i, p: (pick(i, p), 0)),
        ],
    )
    return pl.pallas_call(
        rest_kernel,
        grid_spec=grid_spec,
        out_shape=[out, out],
        cost_estimate=cost,
        compiler_params=pltpu.CompilerParams(vmem_limit_bytes=48 * 1024 * 1024),
    )(pair, rows, m, mw, sw, sh)


def doubling_gather(block, axis):
    size = lax.axis_size(axis)
    me = lax.axis_index(axis)
    bits = size.bit_length() - 1
    low = list(range(bits - 1))[::-1]
    order = low + [bits - 1] if bits > 1 else [0]
    held = block[None]
    for bit in order:
        stride = 1 << bit
        route = [(i, i ^ stride) for i in range(size)]
        other = lax.ppermute(held, axis, route)
        held = place_pair(held, other, me, bit)
    return unpermute(held, order, size, block)


def place_pair(held, other, me, bit):
    mine_low = ((me >> bit) & 1) == 0
    return jnp.where(mine_low, jnp.stack([held, other]), jnp.stack([other, held]))


def unpermute(held, order, size, block):
    bits = len(order)
    placed = order[::-1]
    perm = [placed.index(bits - 1 - j) for j in range(bits)]
    held = held.reshape((2,) * bits + block.shape)
    held = jnp.transpose(held, perm + [bits + k for k in range(block.ndim)])
    return held.reshape((size * block.shape[0],) + block.shape[1:])


BLK_AXES = ("x_hi", "y", "core")
WIDE_AXES = ("x_lo", "z")


def body(series, scrub_mask, seed_index):
    row_count, frames = series.shape
    local_rows = seed_index % row_count
    own_seeds = jnp.take(series, local_rows, axis=0)
    weight = scrub_mask.astype(jnp.float32)
    gathered = lax.all_gather(series, BLK_AXES, axis=0, tiled=True)
    panel_rows = lax.all_gather(own_seeds, "z", axis=0, tiled=True)
    panel_rows = lax.all_gather(panel_rows, "x_lo", axis=0, tiled=True)
    mw = window_masks(weight, frames)
    m = weight[None, :]
    sw, sh = seed_rows(panel_rows, m, mw)
    seeds = panel_rows.shape[0]
    blocks = 1
    for a in BLK_AXES:
        blocks *= lax.axis_size(a)
    core = lax.axis_index("core")
    partner = lax.ppermute(series, "core", [(0, 1), (1, 0)])
    first = core == 0
    pair_rows = jnp.concatenate(
        [jnp.where(first, series, partner), jnp.where(first, partner, series)]
    )
    pair_d, pair_s = compare_rows(pair_rows, m, mw, sw, sh, row_count)
    me = lax.axis_index(BLK_AXES)
    pair = (me - core).astype(jnp.int32)
    rest_d, rest_s = compare_rest(gathered, pair[None], m, mw, sw, sh, row_count, 2)
    start = pair * row_count
    dispersion = lax.dynamic_update_slice(rest_d, pair_d, (start, 0))
    statistic = lax.dynamic_update_slice(rest_s, pair_s, (start, 0))
    shape = (blocks, row_count, seeds)
    return (dispersion.reshape(shape), statistic.reshape(shape))


def solution(mesh):
    from jax.sharding import Mesh
    split = Mesh(mesh.devices.reshape(2, 4, 2, 2, 16), BLK_AXES + WIDE_AXES)
    every = BLK_AXES + WIDE_AXES
    in_specs = (P(every, None), P(), P(every))
    out_specs = (P(None, WIDE_AXES, BLK_AXES), P(None, WIDE_AXES, BLK_AXES))
    return jax.shard_map(body, mesh=split, in_specs=in_specs, out_specs=out_specs, check_vma=False)
```

```python
import numpy as np
import jax
import jax.numpy as jnp
from jax import lax
from jax.experimental import pallas as pl
from jax.experimental.pallas import tpu as pltpu
from jax.sharding import PartitionSpec as P

WIN = 60
STRIDE = 30
NWIN = 20
LANES = 128
SPAN = 256
ROW_TILE = 16
NT = (((1,), (1,)), ((), ()))
HALF_LN2 = 0.5 * float(np.log(2.0))


EPSILON = 1e-05
CLIP_LEVEL = 0.99


def fisher_of(values):
    clipped = jnp.clip(values, -CLIP_LEVEL, CLIP_LEVEL)
    return 0.5 * (jnp.log(1.0 + clipped) - jnp.log(1.0 - clipped))


def window_frames(frames):
    out = []
    for n in range(NWIN):
        start = LANES * ((STRIDE * n) // LANES)
        width = LANES if STRIDE * n - start + WIN <= LANES else SPAN
        out.append((start, min(width, frames - start)))
    return out


def prepare(raw_rows, scrub_mask):
    values = raw_rows.astype(jnp.float32)
    row_count = values.shape[0]
    weight = scrub_mask.astype(jnp.float32)
    covered = STRIDE * (NWIN + 1)
    pieces = values[:, :covered].reshape(row_count, NWIN + 1, STRIDE)
    framed = jnp.concatenate([pieces[:, :-1], pieces[:, 1:]], axis=2)
    mask_pieces = weight[:covered].reshape(NWIN + 1, STRIDE)
    mask_framed = jnp.concatenate([mask_pieces[:-1], mask_pieces[1:]], axis=1)
    valid_count = jnp.sum(mask_framed, axis=1)
    centre = jnp.sum(framed * mask_framed, axis=2) / valid_count
    centred = (framed - centre[:, :, None]) * mask_framed
    spread = jnp.sum(centred * centred, axis=2)
    windows = (centred * lax.rsqrt(spread + EPSILON)[:, :, None]).astype(jnp.bfloat16)
    total_valid = jnp.sum(weight)
    mean_all = jnp.sum(values * weight, axis=1) / total_valid
    centred_all = (values - mean_all[:, None]) * weight
    spread_all = jnp.sum(centred_all * centred_all, axis=1)
    whole_std = (centred_all * lax.rsqrt(spread_all + EPSILON)[:, None]).astype(jnp.bfloat16)
    return (windows, whole_std)


def seed_operands(seed_window, seed_whole, frames):
    blocks = []
    for n, (start, width) in enumerate(window_frames(frames)):
        left = STRIDE * n - start
        part = seed_window[:, n, :]
        part = jnp.pad(part, ((0, 0), (left, SPAN - WIN - left)))
        blocks.append(part.T)
    return jnp.stack(blocks), seed_whole.T


def window_masks(weight, frames):
    padded = jnp.pad(weight, (0, SPAN))
    rows = []
    for n, (start, width) in enumerate(window_frames(frames)):
        local = np.arange(SPAN) + start
        inside = (local >= STRIDE * n) & (local < STRIDE * n + WIN)
        rows.append(padded[start:start + SPAN] * inside.astype(np.float32))
    return jnp.stack(rows)


def compare_kernel(x_ref, m_ref, mw_ref, sw_ref, sh_ref, disp_ref, stat_ref):
    frames = x_ref.shape[1]
    x = x_ref[...].astype(jnp.float32)
    m = m_ref[...]
    total_valid = jnp.sum(m)
    mean_all = jnp.sum(x * m, axis=1, keepdims=True) / total_valid
    centred = (x - mean_all) * m
    spread = jnp.sum(centred * centred, axis=1, keepdims=True)
    whole = (centred * lax.rsqrt(spread + EPSILON)).astype(jnp.bfloat16)
    q = lax.dot_general(whole, sh_ref[...], NT, preferred_element_type=jnp.float32)
    stat_ref[...] = (jnp.sqrt(total_valid - 3.0) * fisher_of(q)).astype(stat_ref.dtype)
    first = None
    second = None
    for n, (start, width) in enumerate(window_frames(frames)):
        xw = x[:, start:start + width]
        mw = mw_ref[n:n + 1, :width]
        count = jnp.sum(mw)
        centre = jnp.sum(xw * mw, axis=1, keepdims=True) / count
        cw = (xw - centre) * mw
        sp = jnp.sum(cw * cw, axis=1, keepdims=True)
        w = (cw * lax.rsqrt(sp + EPSILON)).astype(jnp.bfloat16)
        r = lax.dot_general(w, sw_ref[n, :, :width], NT, preferred_element_type=jnp.float32)
        clipped = jnp.clip(r, -CLIP_LEVEL, CLIP_LEVEL)
        z2 = lax.log2(1.0 + clipped) - lax.log2(1.0 - clipped)
        if first is None:
            first, second = z2, z2 * z2
        else:
            first, second = first + z2, second + z2 * z2
    first = first * (HALF_LN2 / NWIN)
    second = second * (HALF_LN2 * HALF_LN2 / NWIN)
    disp_ref[...] = ((WIN - 3) * (second - first * first)).astype(disp_ref.dtype)


def seed_kernel(x_ref, m_ref, mw_ref, sw_ref, sh_ref):
    frames = x_ref.shape[1]
    x = x_ref[...].astype(jnp.float32)
    m = m_ref[...]
    total_valid = jnp.sum(m)
    mean_all = jnp.sum(x * m, axis=1, keepdims=True) / total_valid
    centred = (x - mean_all) * m
    spread = jnp.sum(centred * centred, axis=1, keepdims=True)
    sh_ref[...] = (centred * lax.rsqrt(spread + EPSILON)).astype(sh_ref.dtype)
    for n, (start, width) in enumerate(window_frames(frames)):
        xw = x[:, start:start + width]
        mw = mw_ref[n:n + 1, :width]
        count = jnp.sum(mw)
        centre = jnp.sum(xw * mw, axis=1, keepdims=True) / count
        cw = (xw - centre) * mw
        sp = jnp.sum(cw * cw, axis=1, keepdims=True)
        sw_ref[n, :, :width] = (cw * lax.rsqrt(sp + EPSILON)).astype(sw_ref.dtype)
        if width < SPAN:
            sw_ref[n, :, width:] = jnp.zeros((x.shape[0], SPAN - width), sw_ref.dtype)


def seed_rows(rows, m, mw):
    seeds, frames = rows.shape
    vmem = pl.BlockSpec(memory_space=pltpu.VMEM)
    return pl.pallas_call(
        seed_kernel,
        in_specs=[vmem, vmem, vmem],
        out_specs=[vmem, vmem],
        out_shape=[
            jax.ShapeDtypeStruct((NWIN, seeds, SPAN), jnp.bfloat16),
            jax.ShapeDtypeStruct((seeds, frames), jnp.bfloat16),
        ],
    )(rows, m, mw)


def compare_rows(rows, m, mw, sw, sh, block):
    count, frames = rows.shape
    seeds = sh.shape[0]
    steps = count // block
    cost = pl.CostEstimate(
        flops=2 * count * seeds * (frames + NWIN * SPAN),
        transcendentals=2 * count * seeds * (NWIN + 1),
        bytes_accessed=count * frames * 2 + sw.size * 2 + 2 * count * seeds * 2,
    )
    out = jax.ShapeDtypeStruct((count, seeds), jnp.bfloat16)
    return pl.pallas_call(
        compare_kernel,
        grid=(steps,),
        in_specs=[
            pl.BlockSpec((block, frames), lambda i: (i, 0)),
            pl.BlockSpec((1, frames), lambda i: (0, 0)),
            pl.BlockSpec((NWIN, SPAN), lambda i: (0, 0)),
            pl.BlockSpec((NWIN, seeds, SPAN), lambda i: (0, 0, 0)),
            pl.BlockSpec((seeds, frames), lambda i: (0, 0)),
        ],
        out_specs=[
            pl.BlockSpec((block, seeds), lambda i: (i, 0)),
            pl.BlockSpec((block, seeds), lambda i: (i, 0)),
        ],
        out_shape=[out, out],
        cost_estimate=cost,
        compiler_params=pltpu.CompilerParams(vmem_limit_bytes=48 * 1024 * 1024),
    )(rows, m, mw, sw, sh)


def rest_kernel(p_ref, x_ref, m_ref, mw_ref, sw_ref, sh_ref, disp_ref, stat_ref):
    compare_kernel(x_ref, m_ref, mw_ref, sw_ref, sh_ref, disp_ref, stat_ref)


def compare_rest(rows, pair, m, mw, sw, sh, block, skip):
    count, frames = rows.shape
    seeds = sh.shape[0]
    steps = count // block - skip

    def pick(i, p):
        return jnp.where(i >= p[0], i + skip, i)

    cost = pl.CostEstimate(
        flops=2 * steps * block * seeds * (frames + NWIN * SPAN),
        transcendentals=2 * steps * block * seeds * (NWIN + 1),
        bytes_accessed=steps * block * (frames + 2 * seeds) * 2 + sw.size * 2,
    )
    out = jax.ShapeDtypeStruct((count, seeds), jnp.bfloat16)
    grid_spec = pltpu.PrefetchScalarGridSpec(
        num_scalar_prefetch=1,
        grid=(steps,),
        in_specs=[
            pl.BlockSpec((block, frames), lambda i, p: (pick(i, p), 0)),
            pl.BlockSpec((1, frames), lambda i, p: (0, 0)),
            pl.BlockSpec((NWIN, SPAN), lambda i, p: (0, 0)),
            pl.BlockSpec((NWIN, seeds, SPAN), lambda i, p: (0, 0, 0)),
            pl.BlockSpec((seeds, frames), lambda i, p: (0, 0)),
        ],
        out_specs=[
            pl.BlockSpec((block, seeds), lambda i, p: (pick(i, p), 0)),
            pl.BlockSpec((block, seeds), lambda i, p: (pick(i, p), 0)),
        ],
    )
    return pl.pallas_call(
        rest_kernel,
        grid_spec=grid_spec,
        out_shape=[out, out],
        cost_estimate=cost,
        compiler_params=pltpu.CompilerParams(vmem_limit_bytes=48 * 1024 * 1024),
    )(pair, rows, m, mw, sw, sh)


def doubling_gather(block, axis):
    size = lax.axis_size(axis)
    me = lax.axis_index(axis)
    bits = size.bit_length() - 1
    low = list(range(bits - 1))[::-1]
    order = low + [bits - 1] if bits > 1 else [0]
    held = block[None]
    for bit in order:
        stride = 1 << bit
        route = [(i, i ^ stride) for i in range(size)]
        other = lax.ppermute(held, axis, route)
        held = place_pair(held, other, me, bit)
    return unpermute(held, order, size, block)


def place_pair(held, other, me, bit):
    mine_low = ((me >> bit) & 1) == 0
    return jnp.where(mine_low, jnp.stack([held, other]), jnp.stack([other, held]))


def unpermute(held, order, size, block):
    bits = len(order)
    placed = order[::-1]
    perm = [placed.index(bits - 1 - j) for j in range(bits)]
    held = held.reshape((2,) * bits + block.shape)
    held = jnp.transpose(held, perm + [bits + k for k in range(block.ndim)])
    return held.reshape((size * block.shape[0],) + block.shape[1:])


BLK_AXES = ("x_hi", "y", "core")
WIDE_AXES = ("x_lo", "z")


def body(series, scrub_mask, seed_index):
    row_count, frames = series.shape
    local_rows = seed_index % row_count
    own_seeds = jnp.take(series, local_rows, axis=0)
    weight = scrub_mask.astype(jnp.float32)
    gathered = lax.all_gather(series, BLK_AXES, axis=0, tiled=True)
    panel_rows = lax.all_gather(own_seeds, "z", axis=0, tiled=True)
    panel_rows = lax.all_gather(panel_rows, "x_lo", axis=0, tiled=True)
    mw = window_masks(weight, frames)
    m = weight[None, :]
    sw, sh = seed_rows(panel_rows, m, mw)
    seeds = panel_rows.shape[0]
    blocks = 1
    for a in BLK_AXES:
        blocks *= lax.axis_size(a)
    near = ("y", "core")
    near_size = lax.axis_size("y") * lax.axis_size("core")
    mine = lax.axis_index(near)
    group = min(4, near_size)
    moved = [series]
    for flip in range(1, group):
        route = [(i, i ^ flip) for i in range(near_size)]
        moved.append(lax.ppermute(series, near, route))
    local = mine % group
    near_rows = jnp.take(jnp.stack(moved), jnp.arange(group) ^ local, axis=0)
    pair_d, pair_s = compare_rows(near_rows.reshape(-1, frames), m, mw, sw, sh, row_count)
    me = lax.axis_index(BLK_AXES)
    pair = (me - local).astype(jnp.int32)
    rest_d, rest_s = compare_rest(gathered, pair[None], m, mw, sw, sh, row_count, group)
    start = pair * row_count
    dispersion = lax.dynamic_update_slice(rest_d, pair_d, (start, 0))
    statistic = lax.dynamic_update_slice(rest_s, pair_s, (start, 0))
    shape = (blocks, row_count, seeds)
    return (dispersion.reshape(shape), statistic.reshape(shape))


def solution(mesh):
    from jax.sharding import Mesh
    split = Mesh(mesh.devices.reshape(2, 4, 2, 2, 16), BLK_AXES + WIDE_AXES)
    every = BLK_AXES + WIDE_AXES
    in_specs = (P(every, None), P(), P(every))
    out_specs = (P(None, WIDE_AXES, BLK_AXES), P(None, WIDE_AXES, BLK_AXES))
    return jax.shard_map(body, mesh=split, in_specs=in_specs, out_specs=out_specs, check_vma=False)
```

```python
import numpy as np
import jax
import jax.numpy as jnp
from jax import lax
from jax.experimental import pallas as pl
from jax.experimental.pallas import tpu as pltpu
from jax.sharding import PartitionSpec as P

WIN = 60
STRIDE = 30
NWIN = 20
LANES = 128
SPAN = 256
ROW_TILE = 16
NT = (((1,), (1,)), ((), ()))
HALF_LN2 = 0.5 * float(np.log(2.0))


EPSILON = 1e-05
CLIP_LEVEL = 0.99


def fisher_of(values):
    clipped = jnp.clip(values, -CLIP_LEVEL, CLIP_LEVEL)
    return 0.5 * (jnp.log(1.0 + clipped) - jnp.log(1.0 - clipped))


def window_frames(frames):
    out = []
    for n in range(NWIN):
        start = LANES * ((STRIDE * n) // LANES)
        width = LANES if STRIDE * n - start + WIN <= LANES else SPAN
        out.append((start, min(width, frames - start)))
    return out


def prepare(raw_rows, scrub_mask):
    values = raw_rows.astype(jnp.float32)
    row_count = values.shape[0]
    weight = scrub_mask.astype(jnp.float32)
    covered = STRIDE * (NWIN + 1)
    pieces = values[:, :covered].reshape(row_count, NWIN + 1, STRIDE)
    framed = jnp.concatenate([pieces[:, :-1], pieces[:, 1:]], axis=2)
    mask_pieces = weight[:covered].reshape(NWIN + 1, STRIDE)
    mask_framed = jnp.concatenate([mask_pieces[:-1], mask_pieces[1:]], axis=1)
    valid_count = jnp.sum(mask_framed, axis=1)
    centre = jnp.sum(framed * mask_framed, axis=2) / valid_count
    centred = (framed - centre[:, :, None]) * mask_framed
    spread = jnp.sum(centred * centred, axis=2)
    windows = (centred * lax.rsqrt(spread + EPSILON)[:, :, None]).astype(jnp.bfloat16)
    total_valid = jnp.sum(weight)
    mean_all = jnp.sum(values * weight, axis=1) / total_valid
    centred_all = (values - mean_all[:, None]) * weight
    spread_all = jnp.sum(centred_all * centred_all, axis=1)
    whole_std = (centred_all * lax.rsqrt(spread_all + EPSILON)[:, None]).astype(jnp.bfloat16)
    return (windows, whole_std)


def seed_operands(seed_window, seed_whole, frames):
    blocks = []
    for n, (start, width) in enumerate(window_frames(frames)):
        left = STRIDE * n - start
        part = seed_window[:, n, :]
        part = jnp.pad(part, ((0, 0), (left, SPAN - WIN - left)))
        blocks.append(part.T)
    return jnp.stack(blocks), seed_whole.T


def window_masks(weight, frames):
    padded = jnp.pad(weight, (0, SPAN))
    rows = []
    for n, (start, width) in enumerate(window_frames(frames)):
        local = np.arange(SPAN) + start
        inside = (local >= STRIDE * n) & (local < STRIDE * n + WIN)
        rows.append(padded[start:start + SPAN] * inside.astype(np.float32))
    return jnp.stack(rows)


def compare_kernel(x_ref, m_ref, mw_ref, sw_ref, sh_ref, disp_ref, stat_ref):
    frames = x_ref.shape[1]
    x = x_ref[...].astype(jnp.float32)
    m = m_ref[...]
    total_valid = jnp.sum(m)
    mean_all = jnp.sum(x * m, axis=1, keepdims=True) / total_valid
    centred = (x - mean_all) * m
    spread = jnp.sum(centred * centred, axis=1, keepdims=True)
    whole = (centred * lax.rsqrt(spread + EPSILON)).astype(jnp.bfloat16)
    q = lax.dot_general(whole, sh_ref[...], NT, preferred_element_type=jnp.float32)
    stat_ref[...] = (jnp.sqrt(total_valid - 3.0) * fisher_of(q)).astype(stat_ref.dtype)
    first = None
    second = None
    for n, (start, width) in enumerate(window_frames(frames)):
        xw = x[:, start:start + width]
        mw = mw_ref[n:n + 1, :width]
        count = jnp.sum(mw)
        centre = jnp.sum(xw * mw, axis=1, keepdims=True) / count
        cw = (xw - centre) * mw
        sp = jnp.sum(cw * cw, axis=1, keepdims=True)
        w = (cw * lax.rsqrt(sp + EPSILON)).astype(jnp.bfloat16)
        r = lax.dot_general(w, sw_ref[n, :, :width], NT, preferred_element_type=jnp.float32)
        clipped = jnp.clip(r, -CLIP_LEVEL, CLIP_LEVEL)
        z2 = lax.log2(1.0 + clipped) - lax.log2(1.0 - clipped)
        if first is None:
            first, second = z2, z2 * z2
        else:
            first, second = first + z2, second + z2 * z2
    first = first * (HALF_LN2 / NWIN)
    second = second * (HALF_LN2 * HALF_LN2 / NWIN)
    disp_ref[...] = ((WIN - 3) * (second - first * first)).astype(disp_ref.dtype)


def seed_kernel(x_ref, m_ref, mw_ref, sw_ref, sh_ref):
    frames = x_ref.shape[1]
    x = x_ref[...].astype(jnp.float32)
    m = m_ref[...]
    total_valid = jnp.sum(m)
    mean_all = jnp.sum(x * m, axis=1, keepdims=True) / total_valid
    centred = (x - mean_all) * m
    spread = jnp.sum(centred * centred, axis=1, keepdims=True)
    sh_ref[...] = (centred * lax.rsqrt(spread + EPSILON)).astype(sh_ref.dtype)
    for n, (start, width) in enumerate(window_frames(frames)):
        xw = x[:, start:start + width]
        mw = mw_ref[n:n + 1, :width]
        count = jnp.sum(mw)
        centre = jnp.sum(xw * mw, axis=1, keepdims=True) / count
        cw = (xw - centre) * mw
        sp = jnp.sum(cw * cw, axis=1, keepdims=True)
        sw_ref[n, :, :width] = (cw * lax.rsqrt(sp + EPSILON)).astype(sw_ref.dtype)
        if width < SPAN:
            sw_ref[n, :, width:] = jnp.zeros((x.shape[0], SPAN - width), sw_ref.dtype)


def seed_rows(rows, m, mw):
    seeds, frames = rows.shape
    vmem = pl.BlockSpec(memory_space=pltpu.VMEM)
    return pl.pallas_call(
        seed_kernel,
        in_specs=[vmem, vmem, vmem],
        out_specs=[vmem, vmem],
        out_shape=[
            jax.ShapeDtypeStruct((NWIN, seeds, SPAN), jnp.bfloat16),
            jax.ShapeDtypeStruct((seeds, frames), jnp.bfloat16),
        ],
    )(rows, m, mw)


def compare_rows(rows, m, mw, sw, sh, block):
    count, frames = rows.shape
    seeds = sh.shape[0]
    steps = count // block
    cost = pl.CostEstimate(
        flops=2 * count * seeds * (frames + NWIN * SPAN),
        transcendentals=2 * count * seeds * (NWIN + 1),
        bytes_accessed=count * frames * 2 + sw.size * 2 + 2 * count * seeds * 2,
    )
    out = jax.ShapeDtypeStruct((count, seeds), jnp.bfloat16)
    return pl.pallas_call(
        compare_kernel,
        grid=(steps,),
        in_specs=[
            pl.BlockSpec((block, frames), lambda i: (i, 0)),
            pl.BlockSpec((1, frames), lambda i: (0, 0)),
            pl.BlockSpec((NWIN, SPAN), lambda i: (0, 0)),
            pl.BlockSpec((NWIN, seeds, SPAN), lambda i: (0, 0, 0)),
            pl.BlockSpec((seeds, frames), lambda i: (0, 0)),
        ],
        out_specs=[
            pl.BlockSpec((block, seeds), lambda i: (i, 0)),
            pl.BlockSpec((block, seeds), lambda i: (i, 0)),
        ],
        out_shape=[out, out],
        cost_estimate=cost,
        compiler_params=pltpu.CompilerParams(vmem_limit_bytes=48 * 1024 * 1024),
    )(rows, m, mw, sw, sh)


def rest_kernel(p_ref, x_ref, m_ref, mw_ref, sw_ref, sh_ref, disp_ref, stat_ref):
    compare_kernel(x_ref, m_ref, mw_ref, sw_ref, sh_ref, disp_ref, stat_ref)


def compare_rest(rows, pair, m, mw, sw, sh, block, skip):
    count, frames = rows.shape
    seeds = sh.shape[0]
    steps = count // block - skip

    def pick(i, p):
        return jnp.where(i >= p[0], i + skip, i)

    cost = pl.CostEstimate(
        flops=2 * steps * block * seeds * (frames + NWIN * SPAN),
        transcendentals=2 * steps * block * seeds * (NWIN + 1),
        bytes_accessed=steps * block * (frames + 2 * seeds) * 2 + sw.size * 2,
    )
    out = jax.ShapeDtypeStruct((count, seeds), jnp.bfloat16)
    grid_spec = pltpu.PrefetchScalarGridSpec(
        num_scalar_prefetch=1,
        grid=(steps,),
        in_specs=[
            pl.BlockSpec((block, frames), lambda i, p: (pick(i, p), 0)),
            pl.BlockSpec((1, frames), lambda i, p: (0, 0)),
            pl.BlockSpec((NWIN, SPAN), lambda i, p: (0, 0)),
            pl.BlockSpec((NWIN, seeds, SPAN), lambda i, p: (0, 0, 0)),
            pl.BlockSpec((seeds, frames), lambda i, p: (0, 0)),
        ],
        out_specs=[
            pl.BlockSpec((block, seeds), lambda i, p: (pick(i, p), 0)),
            pl.BlockSpec((block, seeds), lambda i, p: (pick(i, p), 0)),
        ],
    )
    return pl.pallas_call(
        rest_kernel,
        grid_spec=grid_spec,
        out_shape=[out, out],
        cost_estimate=cost,
        compiler_params=pltpu.CompilerParams(vmem_limit_bytes=48 * 1024 * 1024),
    )(pair, rows, m, mw, sw, sh)


def doubling_gather(block, axis):
    size = lax.axis_size(axis)
    me = lax.axis_index(axis)
    bits = size.bit_length() - 1
    low = list(range(bits - 1))[::-1]
    order = low + [bits - 1] if bits > 1 else [0]
    held = block[None]
    for bit in order:
        stride = 1 << bit
        route = [(i, i ^ stride) for i in range(size)]
        other = lax.ppermute(held, axis, route)
        held = place_pair(held, other, me, bit)
    return unpermute(held, order, size, block)


def place_pair(held, other, me, bit):
    mine_low = ((me >> bit) & 1) == 0
    return jnp.where(mine_low, jnp.stack([held, other]), jnp.stack([other, held]))


def unpermute(held, order, size, block):
    bits = len(order)
    placed = order[::-1]
    perm = [placed.index(bits - 1 - j) for j in range(bits)]
    held = held.reshape((2,) * bits + block.shape)
    held = jnp.transpose(held, perm + [bits + k for k in range(block.ndim)])
    return held.reshape((size * block.shape[0],) + block.shape[1:])


BLK_AXES = ("x_hi", "y", "core")
WIDE_AXES = ("x_lo", "z")


def body(series, scrub_mask, seed_index):
    row_count, frames = series.shape
    local_rows = seed_index % row_count
    own_seeds = jnp.take(series, local_rows, axis=0)
    weight = scrub_mask.astype(jnp.float32)
    gathered = lax.all_gather(series, BLK_AXES, axis=0, tiled=True)
    panel_rows = lax.all_gather(own_seeds, "z", axis=0, tiled=True)
    panel_rows = lax.all_gather(panel_rows, "x_lo", axis=0, tiled=True)
    mw = window_masks(weight, frames)
    m = weight[None, :]
    sw, sh = seed_rows(panel_rows, m, mw)
    seeds = panel_rows.shape[0]
    blocks = 1
    for a in BLK_AXES:
        blocks *= lax.axis_size(a)
    near = ("y", "core")
    near_size = lax.axis_size("y") * lax.axis_size("core")
    mine = lax.axis_index(near)
    group = min(4, near_size)
    late, panel_rows = lax.optimization_barrier((series, panel_rows))
    moved = [series]
    for flip in range(1, group):
        route = [(i, i ^ flip) for i in range(near_size)]
        moved.append(lax.ppermute(late, near, route))
    local = mine % group
    near_rows = jnp.take(jnp.stack(moved), jnp.arange(group) ^ local, axis=0)
    pair_d, pair_s = compare_rows(near_rows.reshape(-1, frames), m, mw, sw, sh, row_count)
    me = lax.axis_index(BLK_AXES)
    pair = (me - local).astype(jnp.int32)
    rest_d, rest_s = compare_rest(gathered, pair[None], m, mw, sw, sh, row_count, group)
    start = pair * row_count
    dispersion = lax.dynamic_update_slice(rest_d, pair_d, (start, 0))
    statistic = lax.dynamic_update_slice(rest_s, pair_s, (start, 0))
    shape = (blocks, row_count, seeds)
    return (dispersion.reshape(shape), statistic.reshape(shape))


def solution(mesh):
    from jax.sharding import Mesh
    split = Mesh(mesh.devices.reshape(2, 4, 2, 2, 16), BLK_AXES + WIDE_AXES)
    every = BLK_AXES + WIDE_AXES
    in_specs = (P(every, None), P(), P(every))
    out_specs = (P(None, WIDE_AXES, BLK_AXES), P(None, WIDE_AXES, BLK_AXES))
    return jax.shard_map(body, mesh=split, in_specs=in_specs, out_specs=out_specs, check_vma=False)
```

```python
import numpy as np
import jax
import jax.numpy as jnp
from jax import lax
from jax.experimental import pallas as pl
from jax.experimental.pallas import tpu as pltpu
from jax.sharding import PartitionSpec as P

WIN = 60
STRIDE = 30
NWIN = 20
LANES = 128
SPAN = 256
ROW_TILE = 16
NT = (((1,), (1,)), ((), ()))
HALF_LN2 = 0.5 * float(np.log(2.0))


EPSILON = 1e-05
CLIP_LEVEL = 0.99


def fisher_of(values):
    clipped = jnp.clip(values, -CLIP_LEVEL, CLIP_LEVEL)
    return 0.5 * (jnp.log(1.0 + clipped) - jnp.log(1.0 - clipped))


def window_frames(frames):
    out = []
    for n in range(NWIN):
        start = LANES * ((STRIDE * n) // LANES)
        width = LANES if STRIDE * n - start + WIN <= LANES else SPAN
        out.append((start, min(width, frames - start)))
    return out


def prepare(raw_rows, scrub_mask):
    values = raw_rows.astype(jnp.float32)
    row_count = values.shape[0]
    weight = scrub_mask.astype(jnp.float32)
    covered = STRIDE * (NWIN + 1)
    pieces = values[:, :covered].reshape(row_count, NWIN + 1, STRIDE)
    framed = jnp.concatenate([pieces[:, :-1], pieces[:, 1:]], axis=2)
    mask_pieces = weight[:covered].reshape(NWIN + 1, STRIDE)
    mask_framed = jnp.concatenate([mask_pieces[:-1], mask_pieces[1:]], axis=1)
    valid_count = jnp.sum(mask_framed, axis=1)
    centre = jnp.sum(framed * mask_framed, axis=2) / valid_count
    centred = (framed - centre[:, :, None]) * mask_framed
    spread = jnp.sum(centred * centred, axis=2)
    windows = (centred * lax.rsqrt(spread + EPSILON)[:, :, None]).astype(jnp.bfloat16)
    total_valid = jnp.sum(weight)
    mean_all = jnp.sum(values * weight, axis=1) / total_valid
    centred_all = (values - mean_all[:, None]) * weight
    spread_all = jnp.sum(centred_all * centred_all, axis=1)
    whole_std = (centred_all * lax.rsqrt(spread_all + EPSILON)[:, None]).astype(jnp.bfloat16)
    return (windows, whole_std)


def seed_operands(seed_window, seed_whole, frames):
    blocks = []
    for n, (start, width) in enumerate(window_frames(frames)):
        left = STRIDE * n - start
        part = seed_window[:, n, :]
        part = jnp.pad(part, ((0, 0), (left, SPAN - WIN - left)))
        blocks.append(part.T)
    return jnp.stack(blocks), seed_whole.T


def window_masks(weight, frames):
    padded = jnp.pad(weight, (0, SPAN))
    rows = []
    for n, (start, width) in enumerate(window_frames(frames)):
        local = np.arange(SPAN) + start
        inside = (local >= STRIDE * n) & (local < STRIDE * n + WIN)
        rows.append(padded[start:start + SPAN] * inside.astype(np.float32))
    return jnp.stack(rows)


def compare_kernel(x_ref, m_ref, mw_ref, sw_ref, sh_ref, disp_ref, stat_ref):
    frames = x_ref.shape[1]
    x = x_ref[...].astype(jnp.float32)
    m = m_ref[...]
    total_valid = jnp.sum(m)
    mean_all = jnp.sum(x * m, axis=1, keepdims=True) / total_valid
    centred = (x - mean_all) * m
    spread = jnp.sum(centred * centred, axis=1, keepdims=True)
    whole = (centred * lax.rsqrt(spread + EPSILON)).astype(jnp.bfloat16)
    q = lax.dot_general(whole, sh_ref[...], NT, preferred_element_type=jnp.float32)
    stat_ref[...] = (jnp.sqrt(total_valid - 3.0) * fisher_of(q)).astype(stat_ref.dtype)
    first = None
    second = None
    for n, (start, width) in enumerate(window_frames(frames)):
        xw = x[:, start:start + width]
        mw = mw_ref[n:n + 1, :width]
        count = jnp.sum(mw)
        centre = jnp.sum(xw * mw, axis=1, keepdims=True) / count
        cw = (xw - centre) * mw
        sp = jnp.sum(cw * cw, axis=1, keepdims=True)
        w = (cw * lax.rsqrt(sp + EPSILON)).astype(jnp.bfloat16)
        r = lax.dot_general(w, sw_ref[n, :, :width], NT, preferred_element_type=jnp.float32)
        clipped = jnp.clip(r, -CLIP_LEVEL, CLIP_LEVEL)
        z2 = lax.log2(1.0 + clipped) - lax.log2(1.0 - clipped)
        if first is None:
            first, second = z2, z2 * z2
        else:
            first, second = first + z2, second + z2 * z2
    first = first * (HALF_LN2 / NWIN)
    second = second * (HALF_LN2 * HALF_LN2 / NWIN)
    disp_ref[...] = ((WIN - 3) * (second - first * first)).astype(disp_ref.dtype)


def seed_kernel(x_ref, m_ref, mw_ref, sw_ref, sh_ref):
    frames = x_ref.shape[1]
    x = x_ref[...].astype(jnp.float32)
    m = m_ref[...]
    total_valid = jnp.sum(m)
    mean_all = jnp.sum(x * m, axis=1, keepdims=True) / total_valid
    centred = (x - mean_all) * m
    spread = jnp.sum(centred * centred, axis=1, keepdims=True)
    sh_ref[...] = (centred * lax.rsqrt(spread + EPSILON)).astype(sh_ref.dtype)
    for n, (start, width) in enumerate(window_frames(frames)):
        xw = x[:, start:start + width]
        mw = mw_ref[n:n + 1, :width]
        count = jnp.sum(mw)
        centre = jnp.sum(xw * mw, axis=1, keepdims=True) / count
        cw = (xw - centre) * mw
        sp = jnp.sum(cw * cw, axis=1, keepdims=True)
        sw_ref[n, :, :width] = (cw * lax.rsqrt(sp + EPSILON)).astype(sw_ref.dtype)
        if width < SPAN:
            sw_ref[n, :, width:] = jnp.zeros((x.shape[0], SPAN - width), sw_ref.dtype)


def seed_rows(rows, m, mw):
    seeds, frames = rows.shape
    vmem = pl.BlockSpec(memory_space=pltpu.VMEM)
    return pl.pallas_call(
        seed_kernel,
        in_specs=[vmem, vmem, vmem],
        out_specs=[vmem, vmem],
        out_shape=[
            jax.ShapeDtypeStruct((NWIN, seeds, SPAN), jnp.bfloat16),
            jax.ShapeDtypeStruct((seeds, frames), jnp.bfloat16),
        ],
    )(rows, m, mw)


def compare_rows(rows, m, mw, sw, sh, block):
    count, frames = rows.shape
    seeds = sh.shape[0]
    steps = count // block
    cost = pl.CostEstimate(
        flops=2 * count * seeds * (frames + NWIN * SPAN),
        transcendentals=2 * count * seeds * (NWIN + 1),
        bytes_accessed=count * frames * 2 + sw.size * 2 + 2 * count * seeds * 2,
    )
    out = jax.ShapeDtypeStruct((count, seeds), jnp.bfloat16)
    return pl.pallas_call(
        compare_kernel,
        grid=(steps,),
        in_specs=[
            pl.BlockSpec((block, frames), lambda i: (i, 0)),
            pl.BlockSpec((1, frames), lambda i: (0, 0)),
            pl.BlockSpec((NWIN, SPAN), lambda i: (0, 0)),
            pl.BlockSpec((NWIN, seeds, SPAN), lambda i: (0, 0, 0)),
            pl.BlockSpec((seeds, frames), lambda i: (0, 0)),
        ],
        out_specs=[
            pl.BlockSpec((block, seeds), lambda i: (i, 0)),
            pl.BlockSpec((block, seeds), lambda i: (i, 0)),
        ],
        out_shape=[out, out],
        cost_estimate=cost,
        compiler_params=pltpu.CompilerParams(vmem_limit_bytes=48 * 1024 * 1024),
    )(rows, m, mw, sw, sh)


def rest_kernel(p_ref, x_ref, m_ref, mw_ref, sw_ref, sh_ref, disp_ref, stat_ref):
    compare_kernel(x_ref, m_ref, mw_ref, sw_ref, sh_ref, disp_ref, stat_ref)


def compare_rest(rows, pair, m, mw, sw, sh, block, skip):
    count, frames = rows.shape
    seeds = sh.shape[0]
    steps = count // block - skip

    def pick(i, p):
        return jnp.where(i >= p[0], i + skip, i)

    cost = pl.CostEstimate(
        flops=2 * steps * block * seeds * (frames + NWIN * SPAN),
        transcendentals=2 * steps * block * seeds * (NWIN + 1),
        bytes_accessed=steps * block * (frames + 2 * seeds) * 2 + sw.size * 2,
    )
    out = jax.ShapeDtypeStruct((count, seeds), jnp.bfloat16)
    grid_spec = pltpu.PrefetchScalarGridSpec(
        num_scalar_prefetch=1,
        grid=(steps,),
        in_specs=[
            pl.BlockSpec((block, frames), lambda i, p: (pick(i, p), 0)),
            pl.BlockSpec((1, frames), lambda i, p: (0, 0)),
            pl.BlockSpec((NWIN, SPAN), lambda i, p: (0, 0)),
            pl.BlockSpec((NWIN, seeds, SPAN), lambda i, p: (0, 0, 0)),
            pl.BlockSpec((seeds, frames), lambda i, p: (0, 0)),
        ],
        out_specs=[
            pl.BlockSpec((block, seeds), lambda i, p: (pick(i, p), 0)),
            pl.BlockSpec((block, seeds), lambda i, p: (pick(i, p), 0)),
        ],
    )
    return pl.pallas_call(
        rest_kernel,
        grid_spec=grid_spec,
        out_shape=[out, out],
        cost_estimate=cost,
        compiler_params=pltpu.CompilerParams(vmem_limit_bytes=48 * 1024 * 1024),
    )(pair, rows, m, mw, sw, sh)


def compare_near(rows, local, m, mw, sw, sh, block):
    count, frames = rows.shape
    seeds = sh.shape[0]
    steps = count // block
    out = jax.ShapeDtypeStruct((count, seeds), jnp.bfloat16)
    grid_spec = pltpu.PrefetchScalarGridSpec(
        num_scalar_prefetch=1,
        grid=(steps,),
        in_specs=[
            pl.BlockSpec((block, frames), lambda i, p: (jnp.bitwise_xor(i, p[0]), 0)),
            pl.BlockSpec((1, frames), lambda i, p: (0, 0)),
            pl.BlockSpec((NWIN, SPAN), lambda i, p: (0, 0)),
            pl.BlockSpec((NWIN, seeds, SPAN), lambda i, p: (0, 0, 0)),
            pl.BlockSpec((seeds, frames), lambda i, p: (0, 0)),
        ],
        out_specs=[
            pl.BlockSpec((block, seeds), lambda i, p: (i, 0)),
            pl.BlockSpec((block, seeds), lambda i, p: (i, 0)),
        ],
    )
    return pl.pallas_call(
        rest_kernel,
        grid_spec=grid_spec,
        out_shape=[out, out],
        compiler_params=pltpu.CompilerParams(vmem_limit_bytes=48 * 1024 * 1024),
    )(local, rows, m, mw, sw, sh)


def doubling_gather(block, axis):
    size = lax.axis_size(axis)
    me = lax.axis_index(axis)
    bits = size.bit_length() - 1
    low = list(range(bits - 1))[::-1]
    order = low + [bits - 1] if bits > 1 else [0]
    held = block[None]
    for bit in order:
        stride = 1 << bit
        route = [(i, i ^ stride) for i in range(size)]
        other = lax.ppermute(held, axis, route)
        held = place_pair(held, other, me, bit)
    return unpermute(held, order, size, block)


def place_pair(held, other, me, bit):
    mine_low = ((me >> bit) & 1) == 0
    return jnp.where(mine_low, jnp.stack([held, other]), jnp.stack([other, held]))


def unpermute(held, order, size, block):
    bits = len(order)
    placed = order[::-1]
    perm = [placed.index(bits - 1 - j) for j in range(bits)]
    held = held.reshape((2,) * bits + block.shape)
    held = jnp.transpose(held, perm + [bits + k for k in range(block.ndim)])
    return held.reshape((size * block.shape[0],) + block.shape[1:])


BLK_AXES = ("x_hi", "y", "core")
WIDE_AXES = ("x_lo", "z")


def body(series, scrub_mask, seed_index):
    row_count, frames = series.shape
    local_rows = seed_index % row_count
    own_seeds = jnp.take(series, local_rows, axis=0)
    weight = scrub_mask.astype(jnp.float32)
    gathered = lax.all_gather(series, BLK_AXES, axis=0, tiled=True)
    panel_rows = lax.all_gather(own_seeds, "z", axis=0, tiled=True)
    panel_rows = lax.all_gather(panel_rows, "x_lo", axis=0, tiled=True)
    mw = window_masks(weight, frames)
    m = weight[None, :]
    sw, sh = seed_rows(panel_rows, m, mw)
    seeds = panel_rows.shape[0]
    blocks = 1
    for a in BLK_AXES:
        blocks *= lax.axis_size(a)
    near = ("y", "core")
    near_size = lax.axis_size("y") * lax.axis_size("core")
    mine = lax.axis_index(near)
    group = min(4, near_size)
    moved = [series]
    for flip in range(1, group):
        route = [(i, i ^ flip) for i in range(near_size)]
        moved.append(lax.ppermute(series, near, route))
    local = mine % group
    near_rows = jnp.stack(moved).reshape(-1, frames)
    pair_d, pair_s = compare_near(near_rows, local.astype(jnp.int32)[None], m, mw, sw, sh, row_count)
    me = lax.axis_index(BLK_AXES)
    pair = (me - local).astype(jnp.int32)
    rest_d, rest_s = compare_rest(gathered, pair[None], m, mw, sw, sh, row_count, group)
    start = pair * row_count
    dispersion = lax.dynamic_update_slice(rest_d, pair_d, (start, 0))
    statistic = lax.dynamic_update_slice(rest_s, pair_s, (start, 0))
    shape = (blocks, row_count, seeds)
    return (dispersion.reshape(shape), statistic.reshape(shape))


def solution(mesh):
    from jax.sharding import Mesh
    split = Mesh(mesh.devices.reshape(2, 4, 2, 2, 16), BLK_AXES + WIDE_AXES)
    every = BLK_AXES + WIDE_AXES
    in_specs = (P(every, None), P(), P(every))
    out_specs = (P(None, WIDE_AXES, BLK_AXES), P(None, WIDE_AXES, BLK_AXES))
    return jax.shard_map(body, mesh=split, in_specs=in_specs, out_specs=out_specs, check_vma=False)
```
